32 devices in a mesh: expert: 8 (over z, x), tensor: 4 (over y, core).
Axes of the slice: x: 2, y: 2, z: 4, core: 2. Of those that a mesh axis runs over, the one named last changes fastest.
Arguments:
- context: bfloat16 [2048, 2048], P('expert', 'tensor'), may hold values from -0.25976562 to 0.25976562
- out_proj: bfloat16 [2048, 2048], P('tensor'), may hold values from -0.125 to 0.125
- residual: bfloat16 [2048, 2048], P(('expert', 'tensor')), may hold values from -0.25976562 to 0.25976562
- norm_gain: float32 [2048], replicated, may hold values from 0.1 to 1.9
- router_weight: float32 [2048, 64], replicated, may hold values from -5.524272 to 5.524272
- expert_ids: int32 [2048, 8], P('expert'), may hold values from 0 to 63, all different within a row; in each aligned block of 64 rows (0 to 63, 64 to 127, ...) at most 10 rows name the same one
- placement: int32 [128], replicated, may hold values from 0 to 63, as said below
- expert_weights: bfloat16 [128, 3, 2048, 1024], P('expert', None, None, 'tensor'), as said below
- post_gain: float32 [2048], replicated, may hold values from 0.5 to 1.5
Outputs:
- hidden_out: float32 [2048, 2048], P(('expert', 'tensor'))
- normed_out: float32 [2048, 2048], P(('expert', 'tensor'))
The draws below stay inside these ranges and needn't reach their ends.
Inputs may be any that keep to these rules, and one draw needn't show every extreme that they name: `expert_ids`: each row names 8 different experts. In each aligned block of 64 rows (the rows of one device) no expert is named by more than 10 rows, a bound that some block reaches; every expert is named somewhere. `placement`: every expert is held by one, three or five slots. `expert_weights`: slots that hold the same expert carry equal weights.
All inputs are finite; a program needn't handle non-finite values.
Results may differ from the reference program's by a relative error of at most 0.018.
Values may be sent and summed in bfloat16 or wider, within the bound.
No kernel may reach another device: no remote copies, remote signals or barrier semaphores. Data moves between devices by JAX's collectives and lax.ppermute only.
A program may use at most 256 MiB of HBM per device.

```python
import math
import jax
import jax.numpy as jnp
import numpy as np
from jax import lax

D = 2048
FF = 1024
EXPERTS = 64
TOP = 8
ROWS_DEV = 64
TOKENS = 2048
SLOTS = 128
MOST = 10
N_EXPERT = 8
N_TENSOR = 4


def slot_table(key):
    base_key = jax.random.fold_in(key, 101)
    order_key = jax.random.fold_in(base_key, 1)
    shuffle_key = jax.random.fold_in(base_key, 2)
    hot_count = EXPERTS // 8
    warm_count = EXPERTS // 4
    copies = np.concatenate([np.full(hot_count, 5), np.full(warm_count, 3), np.full(EXPERTS - hot_count - warm_count, 1)])
    rank_list = np.repeat(np.arange(EXPERTS), copies).astype(np.int32)
    popular = jax.random.permutation(order_key, EXPERTS).astype(jnp.int32)
    held_by = popular[jnp.asarray(rank_list)]
    shuffle = jax.random.permutation(shuffle_key, SLOTS).astype(jnp.int32)
    return held_by[shuffle].astype(jnp.int32)


def draw_placement(key, part):
    return slot_table(key)


def draw_expert_weights(key, part):
    held_by = slot_table(key)
    weight_key = jax.random.fold_in(key, 202)
    scales = jnp.array([D ** (-0.5), D ** (-0.5), FF ** (-0.5)], jnp.float32)[:, None, None]

    def one_slot(expert):
        values = jax.random.normal(jax.random.fold_in(weight_key, expert), (3, D, FF), jnp.float32)
        return (values * scales).astype(jnp.bfloat16)
    return lax.map(one_slot, held_by)


def draw_router_weight(key, part):
    base_draw = jnp.clip(jax.random.normal(jax.random.fold_in(key, 303), (D, EXPERTS), jnp.float32), -4.0, 4.0)
    return base_draw * (0.3 * D ** (-0.5))


def level_of(rng, extent, pieces, smallest, top_value):
    factor_of, own = 1.0, jax.random.fold_in(rng, 6)
    for axis_at, blocks in pieces:
        heights = jnp.exp(jax.random.uniform(jax.random.fold_in(own, axis_at), (blocks,), jnp.float32, smallest / len(pieces), top_value / len(pieces)))
        factor_of = factor_of * jnp.repeat(heights, extent[axis_at] // blocks).reshape([-1 if axis == axis_at else 1 for axis in range(len(extent))])
    return factor_of


def shared_out(rng, own, number, rows, count, top, reach, skew):
    ranking = jax.random.permutation(rng, count)
    crowded, usual = portions_of(count, rows * top, reach, skew, True), portions_of(count, rows * top, reach, skew, False)
    places = jnp.arange(count)

    def named(sizes, turn):
        used = int((sizes > 0).sum())
        fixed = max(1, used // 4)
        moved = fixed + (places - fixed + turn * (used - fixed)) % max(1, count - fixed)
        return jnp.zeros((count,), jnp.int32).at[ranking[jnp.where(places < fixed, places, moved)]].set(jnp.asarray(sizes, jnp.int32))

    sizes = jnp.where(number % 4 == 0, named(crowded, number // 4), named(usual, number - number // 4 - 1))
    mixed = jax.random.permutation(jax.random.fold_in(own, 3), count)
    source_of, sink = mixed[0:count // 2 * 2:2], mixed[1:count // 2 * 2:2]
    slack = jnp.minimum(sizes[source_of] - 1, reach - sizes[sink]) // 2
    slack = jnp.where((source_of == ranking[0]) | (sink == ranking[0]) | (sizes[sink] == 0), 0, jnp.maximum(slack, 0))
    moved = jax.random.randint(jax.random.fold_in(own, 4), (count // 2,), 0, 1 << 20) % (slack + 1)
    sizes = sizes.at[source_of].add(-moved).at[sink].add(moved)
    members = jnp.searchsorted(jnp.cumsum(sizes), jnp.arange(rows * top), side="right").astype(jnp.int32)
    grid = members.reshape(top, rows).T
    grid = grid[jax.random.permutation(jax.random.fold_in(own, 1), rows)]
    turn = jax.random.randint(jax.random.fold_in(own, 2), (rows, 1), 0, top)
    return jnp.take_along_axis(grid, (jnp.arange(top)[None, :] + turn) % top, axis=1)


def portions_of(amount, total, most, skew, full):
    portions = [(1 << 20) // math.isqrt(standing ** skew) + 1 for standing in range(1, amount + 1)]
    largest = most if full else min(most, max(-(-total // amount), total * portions[0] // sum(portions)))
    least = 1 if total - largest >= amount - 1 else 0
    given, rest = [largest] + [least] * (amount - 1), total - largest - least * (amount - 1)
    while rest > 0:
        free = [i for i in range(1, amount) if given[i] < largest] or [i for i in range(1, amount) if given[i] < most]
        mass, left = sum([portions[i] for i in free]), rest
        for i in free:
            addition = min(most - given[i], max(1, left * portions[i] // mass), rest)
            given[i] = given[i] + addition
            rest = rest - addition
    return np.array(given)


def gaussian(stream_key, extent, scale, most, pieces=(), kind=jnp.bfloat16):
    level = level_of(stream_key, extent, pieces, -0.22, 0.18) if pieces else 1.0
    values = jax.random.normal(stream_key, extent, jnp.float32) * scale * level
    return jnp.minimum(jnp.maximum(values, -most), most).astype(kind)


def setup_inputs(seed: int = 0) -> dict:
    key_list = jax.random.split(jax.random.key(seed), 10)
    context = jnp.clip(jax.random.uniform(key_list[0], (TOKENS, D), jnp.float32, -0.25976562, 0.25976562) * level_of(key_list[0], (TOKENS, D), ((0, 8), (1, 4)), -0.4, 0.0), -0.25976562, 0.25976562).astype(jnp.bfloat16)
    out_proj = gaussian(key_list[1], (D, D), D ** -0.5, 0.125, ((0, 4),))
    residual = jnp.clip(jax.random.uniform(key_list[2], (TOKENS, D), jnp.float32, -0.25976562, 0.25976562) * level_of(key_list[2], (TOKENS, D), ((0, 32),), -0.4, 0.0), -0.25976562, 0.25976562).astype(jnp.bfloat16)
    norm_gain = jnp.clip(1.0 + 0.18 * jax.random.normal(key_list[3], (D,), jnp.float32), 0.1, 1.9)
    router_weight = draw_router_weight(jax.random.fold_in(key_list[9], 71), 0)
    expert_ids_keys = jax.random.split(jax.random.fold_in(key_list[5], 1), TOKENS // ROWS_DEV)
    expert_ids_turns = jax.random.permutation(jax.random.fold_in(key_list[5], 3), TOKENS // ROWS_DEV)
    expert_ids = jax.vmap(lambda own, number: shared_out(jax.random.fold_in(key_list[5], 2), own, number, ROWS_DEV, EXPERTS, TOP, MOST, 2))(expert_ids_keys, expert_ids_turns).reshape((TOKENS, TOP))
    placement = draw_placement(jax.random.fold_in(key_list[9], 71), 0)
    expert_weights = draw_expert_weights(jax.random.fold_in(key_list[9], 71), 0)
    post_gain = jnp.clip(1.0 + 0.1 * jax.random.normal(key_list[8], (D,), jnp.float32), 0.5, 1.5)
    return dict(context=context, out_proj=out_proj, residual=residual, norm_gain=norm_gain, router_weight=router_weight, expert_ids=expert_ids, placement=placement, expert_weights=expert_weights, post_gain=post_gain)


EPS = 1e-06

def rms_scale(values, gain_row):
    mean_square = lax.optimization_barrier(jnp.mean(values * values, axis=-1, keepdims=True))
    return values * lax.rsqrt(mean_square + EPS) * gain_row

def reference(context, out_proj, residual, norm_gain, router_weight, expert_ids, placement, expert_weights, post_gain):
    d_quarter = D // N_TENSOR
    attention = jnp.zeros((TOKENS, D), jnp.float32)
    for q_index in range(N_TENSOR):
        partial_value = jnp.dot(context[:, q_index * d_quarter:(q_index + 1) * d_quarter], out_proj[q_index * d_quarter:(q_index + 1) * d_quarter], preferred_element_type=jnp.float32)
        partial_value = lax.optimization_barrier(partial_value.astype(jnp.bfloat16))
        attention = attention + partial_value.astype(jnp.float32)
    hidden_mid = residual.astype(jnp.float32) + attention
    normed_full = rms_scale(hidden_mid, norm_gain)
    normed = normed_full.astype(jnp.bfloat16)
    logits = jnp.dot(normed_full, router_weight, precision=lax.Precision.HIGHEST)
    chosen = jnp.take_along_axis(logits, expert_ids, axis=1)
    gate_weights = jax.nn.softmax(chosen, axis=-1)
    expert_range = jnp.arange(EXPERTS, dtype=jnp.int32)
    first_slot = jnp.argmax((placement[None, :] == expert_range[:, None]).astype(jnp.int32), axis=1).astype(jnp.int32)
    flat_experts = expert_ids.reshape(-1)
    count_all = TOKENS * TOP
    onehot = (flat_experts[:, None] == expert_range[None, :]).astype(jnp.int32)
    rank_in = lax.optimization_barrier(jnp.sum(jnp.cumsum(onehot, axis=0) * onehot, axis=1)) - 1
    capacity_all = N_EXPERT * N_TENSOR * MOST
    index_table = jnp.full((EXPERTS * capacity_all,), count_all, jnp.int32)
    index_table = index_table.at[flat_experts * capacity_all + rank_in].set(jnp.arange(count_all, dtype=jnp.int32))
    index_table = index_table.reshape(EXPERTS, capacity_all)
    gates_flat = gate_weights.reshape(-1)
    f_quarter = FF // N_TENSOR

    def per_expert(totals, expert):
        index_row = index_table[expert]
        is_valid = index_row < count_all
        safe_index = jnp.where(is_valid, index_row, 0).astype(jnp.int32)
        token_ids = safe_index // TOP
        weight_row = jnp.where(is_valid, gates_flat[safe_index], 0.0)
        rows_in = normed[token_ids]
        weights = expert_weights[first_slot[expert]]
        gate_pre = jnp.dot(rows_in, weights[0], preferred_element_type=jnp.float32)
        up_pre = jnp.dot(rows_in, weights[1], preferred_element_type=jnp.float32)
        inner_act = (jax.nn.silu(gate_pre) * up_pre).astype(jnp.bfloat16)
        out_sum = jnp.zeros((capacity_all, D), jnp.float32)
        for q_index in range(N_TENSOR):
            partial_value = lax.dot_general(inner_act[:, q_index * f_quarter:(q_index + 1) * f_quarter], weights[2][:, q_index * f_quarter:(q_index + 1) * f_quarter], (((1,), (1,)), ((), ())), preferred_element_type=jnp.float32)
            partial_value = lax.optimization_barrier(partial_value.astype(jnp.bfloat16))
            out_sum = out_sum + partial_value.astype(jnp.float32)
        output = out_sum.astype(jnp.bfloat16)
        totals = totals.at[token_ids].add(weight_row[:, None] * output.astype(jnp.float32))
        return (totals, None)
    moe_sum, unused = lax.scan(per_expert, jnp.zeros((TOKENS, D), jnp.float32), expert_range)
    hidden_out = hidden_mid + moe_sum
    normed_out = rms_scale(hidden_out, post_gain)
    return (hidden_out, normed_out)
```

```python
import jax
import jax.numpy as jnp
from jax import lax
from jax.sharding import PartitionSpec as P

EPS = 1e-06


def rms_scale(values, gain_row):
    mean_square = jnp.mean(values * values, axis=-1, keepdims=True)
    return values * lax.rsqrt(mean_square + EPS) * gain_row


def expert_partial(block_rows, weights):
    gate_pre = jnp.einsum(
        "nqsmd,sdf->nqsmf", block_rows, weights[:, 0], preferred_element_type=jnp.float32
    )
    up_pre = jnp.einsum(
        "nqsmd,sdf->nqsmf", block_rows, weights[:, 1], preferred_element_type=jnp.float32
    )
    inner_act = (jax.nn.silu(gate_pre) * up_pre).astype(jnp.bfloat16)
    return jnp.einsum(
        "nqsmf,sdf->nqsmd", inner_act, weights[:, 2], preferred_element_type=jnp.float32
    )


def on_device(
    context,
    out_proj,
    residual,
    norm_gain,
    router_weight,
    expert_ids,
    placement,
    expert_weights,
    post_gain,
):
    groups = lax.axis_size("tensor")
    holders = lax.axis_size("expert")
    my_group = lax.axis_index("tensor")
    my_holder = lax.axis_index("expert")
    row_count = residual.shape[0]
    model_width = residual.shape[1]
    top_count = expert_ids.shape[1]
    expert_count = router_weight.shape[1]
    slot_dev = expert_weights.shape[0]
    slot_total = placement.shape[0]
    blocks = holders * groups
    capacity = max(2, row_count * top_count * 5 // (expert_count * 4))
    expert_range = jnp.arange(expert_count, dtype=jnp.int32)
    slot_range = jnp.arange(slot_total, dtype=jnp.int32)
    attention = lax.psum_scatter(
        jnp.dot(context, out_proj, preferred_element_type=jnp.float32).astype(jnp.bfloat16),
        "tensor",
        scatter_dimension=0,
        tiled=True,
    ).astype(jnp.float32)
    hidden_mid = residual.astype(jnp.float32) + attention
    normed_full = rms_scale(hidden_mid, norm_gain)
    normed = normed_full.astype(jnp.bfloat16)
    logits = jnp.dot(normed_full, router_weight, precision=lax.Precision.HIGHEST)
    own_ids = lax.dynamic_slice_in_dim(expert_ids, my_group * row_count, row_count, 0)
    own_onehot = own_ids[:, :, None] == expert_range[None, None, :]
    chosen = jnp.sum(jnp.where(own_onehot, logits[:, None, :], 0.0), axis=-1)
    gate_weights = jax.nn.softmax(chosen, axis=-1)
    all_rows = lax.all_gather(normed, ("expert", "tensor"), axis=0, tiled=True)
    all_ids = lax.all_gather(expert_ids, "expert", axis=0, tiled=True)
    holds = (placement[None, :] == expert_range[:, None]).astype(jnp.int32)
    copies = jnp.sum(holds, axis=1)
    copy_rank = jnp.cumsum(holds, axis=1) - 1
    holder_range = jnp.arange(holders, dtype=jnp.int32)
    copy_pick = holder_range[:, None] % copies[None, :]
    picked = (holds[None] > 0) & (copy_rank[None] == copy_pick[:, :, None])
    slot_pick = jnp.sum(jnp.where(picked, slot_range[None, None, :], 0), axis=2)
    flat_ids = all_ids.reshape(blocks, row_count * top_count)
    block_holder = jnp.arange(blocks, dtype=jnp.int32) // groups
    block_pick = slot_pick[block_holder]
    onehot = flat_ids[:, :, None] == expert_range
    slot_of = jnp.sum(jnp.where(onehot, block_pick[:, None, :], 0), axis=-1)
    slot_hot = (slot_of[:, :, None] == slot_range).astype(jnp.int32)
    rank_all = jnp.sum(jnp.cumsum(slot_hot, axis=1) * slot_hot, axis=-1) - 1
    holder_all = slot_of // slot_dev
    local_all = slot_of % slot_dev
    block_ids = jnp.arange(blocks, dtype=jnp.int32)[:, None]
    token_of = block_ids * row_count + jnp.arange(row_count * top_count, dtype=jnp.int32)[None, :] // top_count
    mine = holder_all == my_holder
    row_total = blocks * slot_dev * capacity
    target = jnp.where(mine, (block_ids * slot_dev + local_all) * capacity + rank_all, row_total)
    index_table = jnp.zeros((row_total,), jnp.int32).at[target.reshape(-1)].set(
        token_of.reshape(-1), mode="drop", unique_indices=True
    )
    received = jnp.take(all_rows, index_table, axis=0).reshape(
        holders, groups, slot_dev, capacity, model_width
    )
    own_block = my_holder * groups + my_group
    holder = lax.dynamic_index_in_dim(holder_all, own_block, 0, keepdims=False)
    local_slot = lax.dynamic_index_in_dim(local_all, own_block, 0, keepdims=False)
    rank_in = lax.dynamic_index_in_dim(rank_all, own_block, 0, keepdims=False)
    partial_value = expert_partial(received, expert_weights)
    expert_sum = lax.psum_scatter(
        partial_value.astype(jnp.bfloat16), "tensor", scatter_dimension=1, tiled=True
    )
    returned = lax.all_to_all(expert_sum, "expert", split_axis=0, concat_axis=0, tiled=True)
    own_index = (holder * slot_dev + local_slot) * capacity + rank_in
    outputs = returned.reshape(-1, model_width)[own_index].reshape(
        row_count, top_count, model_width
    )
    moe_sum = jnp.einsum("rk,rkd->rd", gate_weights, outputs.astype(jnp.float32))
    hidden_out = hidden_mid + moe_sum
    normed_out = rms_scale(hidden_out, post_gain)
    return (hidden_out, normed_out)


def solution(mesh):
    in_specs = (
        P("expert", "tensor"),
        P("tensor", None),
        P(("expert", "tensor"), None),
        P(),
        P(),
        P("expert", None),
        P(),
        P("expert", None, None, "tensor"),
        P(),
    )
    out_specs = (P(("expert", "tensor"), None), P(("expert", "tensor"), None))
    return jax.shard_map(
        on_device, mesh=mesh, in_specs=in_specs, out_specs=out_specs, check_vma=False
    )
```

```python
import jax
import jax.numpy as jnp
from jax import lax
from jax.sharding import PartitionSpec as P

EPS = 1e-06


def rms_scale(values, gain_row):
    mean_square = jnp.mean(values * values, axis=-1, keepdims=True)
    return values * lax.rsqrt(mean_square + EPS) * gain_row


def expert_partial(block_rows, weights):
    gate_pre = jnp.einsum(
        "nqsmd,sdf->nqsmf", block_rows, weights[:, 0], preferred_element_type=jnp.float32
    )
    up_pre = jnp.einsum(
        "nqsmd,sdf->nqsmf", block_rows, weights[:, 1], preferred_element_type=jnp.float32
    )
    inner_act = (jax.nn.silu(gate_pre) * up_pre).astype(jnp.bfloat16)
    return jnp.einsum(
        "nqsmf,sdf->nqsmd", inner_act, weights[:, 2], preferred_element_type=jnp.float32
    )


def on_device(
    context,
    out_proj,
    residual,
    norm_gain,
    router_weight,
    expert_ids,
    placement,
    expert_weights,
    post_gain,
):
    groups = lax.axis_size("tensor")
    holders = lax.axis_size("expert")
    my_group = lax.axis_index("tensor")
    my_holder = lax.axis_index("expert")
    row_count = residual.shape[0]
    model_width = residual.shape[1]
    top_count = expert_ids.shape[1]
    expert_count = router_weight.shape[1]
    slot_dev = expert_weights.shape[0]
    slot_total = placement.shape[0]
    blocks = holders * groups
    capacity = max(2, row_count * top_count * 5 // (expert_count * 4))
    expert_range = jnp.arange(expert_count, dtype=jnp.int32)
    slot_range = jnp.arange(slot_total, dtype=jnp.int32)
    attention = lax.psum_scatter(
        jnp.dot(context, out_proj, preferred_element_type=jnp.float32).astype(jnp.bfloat16),
        "tensor",
        scatter_dimension=0,
        tiled=True,
    ).astype(jnp.float32)
    hidden_mid = residual.astype(jnp.float32) + attention
    normed_full = rms_scale(hidden_mid, norm_gain)
    normed = normed_full.astype(jnp.bfloat16)
    logits = jnp.dot(normed_full, router_weight, precision=lax.Precision.HIGHEST)
    own_ids = lax.dynamic_slice_in_dim(expert_ids, my_group * row_count, row_count, 0)
    own_onehot = own_ids[:, :, None] == expert_range[None, None, :]
    chosen = jnp.sum(jnp.where(own_onehot, logits[:, None, :], 0.0), axis=-1)
    gate_weights = jax.nn.softmax(chosen, axis=-1)
    ids_wide = jnp.pad(own_ids.astype(jnp.bfloat16), ((0, 0), (0, 128 - top_count)))
    packed = lax.all_gather(
        jnp.concatenate([normed, ids_wide], axis=1), ("expert", "tensor"), axis=0, tiled=True
    )
    all_rows = packed[:, :model_width]
    all_ids = packed[:, model_width:model_width + top_count].astype(jnp.int32)
    holds = (placement[None, :] == expert_range[:, None]).astype(jnp.int32)
    copies = jnp.sum(holds, axis=1)
    copy_rank = jnp.cumsum(holds, axis=1) - 1
    holder_range = jnp.arange(holders, dtype=jnp.int32)
    copy_pick = holder_range[:, None] % copies[None, :]
    picked = (holds[None] > 0) & (copy_rank[None] == copy_pick[:, :, None])
    slot_pick = jnp.sum(jnp.where(picked, slot_range[None, None, :], 0), axis=2)
    pair_count = row_count * top_count
    flat_ids = all_ids.reshape(blocks, pair_count)
    block_holder = jnp.arange(blocks, dtype=jnp.int32) // groups
    local_pick = jnp.where(
        slot_pick // slot_dev == my_holder, slot_pick % slot_dev, slot_dev
    )[block_holder]
    onehot = flat_ids[:, :, None] == expert_range
    local_all = jnp.sum(jnp.where(onehot, local_pick[:, None, :], 0), axis=-1)
    local_range = jnp.arange(slot_dev, dtype=jnp.int32)
    local_hot = (local_all[:, :, None] == local_range).astype(jnp.int32)
    rank_all = jnp.sum(jnp.cumsum(local_hot, axis=1) * local_hot, axis=-1) - 1
    key = jnp.where(local_all < slot_dev, local_all * capacity + rank_all, -1)
    key = key.reshape(blocks, row_count, top_count)
    pos_range = jnp.arange(slot_dev * capacity, dtype=jnp.int32)
    pick_hot = jnp.any(key[:, :, :, None] == pos_range, axis=2).astype(jnp.bfloat16)
    received = jnp.einsum(
        "buj,bud->bjd",
        pick_hot,
        all_rows.reshape(blocks, row_count, model_width),
        preferred_element_type=jnp.float32,
    ).astype(jnp.bfloat16).reshape(holders, groups, slot_dev, capacity, model_width)
    own_flat = own_ids.reshape(-1)
    own_onehot_flat = own_flat[:, None] == expert_range
    slot_of = jnp.sum(jnp.where(own_onehot_flat, slot_pick[my_holder][None, :], 0), axis=-1)
    slot_hot = (slot_of[:, None] == slot_range).astype(jnp.int32)
    rank_in = jnp.sum(jnp.cumsum(slot_hot, axis=0) * slot_hot, axis=-1) - 1
    holder = slot_of // slot_dev
    local_slot = slot_of % slot_dev
    partial_value = expert_partial(received, expert_weights)
    expert_sum = lax.psum_scatter(
        partial_value.astype(jnp.bfloat16), "tensor", scatter_dimension=1, tiled=True
    )
    returned = lax.all_to_all(expert_sum, "expert", split_axis=0, concat_axis=0, tiled=True)
    own_index = (holder * slot_dev + local_slot) * capacity + rank_in
    outputs = returned.reshape(-1, model_width)[own_index].reshape(
        row_count, top_count, model_width
    )
    moe_sum = jnp.einsum("rk,rkd->rd", gate_weights, outputs.astype(jnp.float32))
    hidden_out = hidden_mid + moe_sum
    normed_out = rms_scale(hidden_out, post_gain)
    return (hidden_out, normed_out)


def solution(mesh):
    in_specs = (
        P("expert", "tensor"),
        P("tensor", None),
        P(("expert", "tensor"), None),
        P(),
        P(),
        P("expert", None),
        P(),
        P("expert", None, None, "tensor"),
        P(),
    )
    out_specs = (P(("expert", "tensor"), None), P(("expert", "tensor"), None))
    return jax.shard_map(
        on_device, mesh=mesh, in_specs=in_specs, out_specs=out_specs, check_vma=False
    )
```

```python
import jax
import jax.numpy as jnp
from jax import lax
from jax.sharding import PartitionSpec as P

EPS = 1e-06


def rms_scale(values, gain_row):
    mean_square = jnp.mean(values * values, axis=-1, keepdims=True)
    return values * lax.rsqrt(mean_square + EPS) * gain_row


def expert_partial(block_rows, weights):
    gate_pre = jnp.einsum(
        "nqsmd,sdf->nqsmf", block_rows, weights[:, 0], preferred_element_type=jnp.float32
    )
    up_pre = jnp.einsum(
        "nqsmd,sdf->nqsmf", block_rows, weights[:, 1], preferred_element_type=jnp.float32
    )
    inner_act = (jax.nn.silu(gate_pre) * up_pre).astype(jnp.bfloat16)
    return jnp.einsum(
        "nqsmf,sdf->nqsmd", inner_act, weights[:, 2], preferred_element_type=jnp.float32
    )


def on_device(
    context,
    out_proj,
    residual,
    norm_gain,
    router_weight,
    expert_ids,
    placement,
    expert_weights,
    post_gain,
):
    groups = lax.axis_size("tensor")
    holders = lax.axis_size("expert")
    my_group = lax.axis_index("tensor")
    my_holder = lax.axis_index("expert")
    row_count = residual.shape[0]
    model_width = residual.shape[1]
    top_count = expert_ids.shape[1]
    expert_count = router_weight.shape[1]
    slot_dev = expert_weights.shape[0]
    slot_total = placement.shape[0]
    blocks = holders * groups
    capacity = max(2, row_count * top_count * 5 // (expert_count * 4))
    expert_range = jnp.arange(expert_count, dtype=jnp.int32)
    slot_range = jnp.arange(slot_total, dtype=jnp.int32)
    attention = lax.psum_scatter(
        jnp.dot(context, out_proj, preferred_element_type=jnp.float32).astype(jnp.bfloat16),
        "tensor",
        scatter_dimension=0,
        tiled=True,
    ).astype(jnp.float32)
    hidden_mid = residual.astype(jnp.float32) + attention
    normed_full = rms_scale(hidden_mid, norm_gain)
    normed = normed_full.astype(jnp.bfloat16)
    logits = jnp.dot(normed_full, router_weight, precision=lax.Precision.HIGHEST)
    own_ids = lax.dynamic_slice_in_dim(expert_ids, my_group * row_count, row_count, 0)
    own_onehot = own_ids[:, :, None] == expert_range[None, None, :]
    chosen = jnp.sum(jnp.where(own_onehot, logits[:, None, :], 0.0), axis=-1)
    gate_weights = jax.nn.softmax(chosen, axis=-1)
    gate_hi = gate_weights.astype(jnp.bfloat16)
    gate_lo = (gate_weights - gate_hi.astype(jnp.float32)).astype(jnp.bfloat16)
    side = jnp.concatenate([own_ids.astype(jnp.bfloat16), gate_hi, gate_lo], axis=1)
    side = jnp.pad(side, ((0, 0), (0, 128 - 3 * top_count)))
    packed = lax.all_gather(
        jnp.concatenate([normed, side], axis=1), ("expert", "tensor"), axis=0, tiled=True
    ).reshape(blocks, row_count, model_width + 128)
    all_rows = packed[:, :, :model_width]
    all_ids = packed[:, :, model_width:model_width + top_count].astype(jnp.int32)
    all_hi = packed[:, :, model_width + top_count:model_width + 2 * top_count]
    all_lo = packed[:, :, model_width + 2 * top_count:model_width + 3 * top_count]
    holds = (placement[None, :] == expert_range[:, None]).astype(jnp.int32)
    copies = jnp.sum(holds, axis=1)
    copy_rank = jnp.cumsum(holds, axis=1) - 1
    holder_range = jnp.arange(holders, dtype=jnp.int32)
    copy_pick = holder_range[:, None] % copies[None, :]
    picked = (holds[None] > 0) & (copy_rank[None] == copy_pick[:, :, None])
    slot_pick = jnp.sum(jnp.where(picked, slot_range[None, None, :], 0), axis=2)
    local_range = jnp.arange(slot_dev, dtype=jnp.int32)
    mine_map = (slot_pick[:, :, None] == my_holder * slot_dev + local_range).astype(jnp.bfloat16)
    block_holder = jnp.arange(blocks, dtype=jnp.int32) // groups
    block_map = mine_map[block_holder]
    names = all_ids[:, :, :, None] == expert_range
    name_hot = jnp.any(names, axis=2).astype(jnp.bfloat16)
    gate_e_hi = jnp.sum(jnp.where(names, all_hi[:, :, :, None], 0), axis=2).astype(jnp.bfloat16)
    gate_e_lo = jnp.sum(jnp.where(names, all_lo[:, :, :, None], 0), axis=2).astype(jnp.bfloat16)
    stack = jnp.concatenate([name_hot, gate_e_hi, gate_e_lo], axis=1)
    per_slot = jnp.einsum("bue,bes->bus", stack, block_map, preferred_element_type=jnp.float32)
    token_hit = per_slot[:, :row_count]
    gate_sel_hi = per_slot[:, row_count:2 * row_count]
    gate_sel_lo = per_slot[:, 2 * row_count:]
    token_range = jnp.arange(row_count, dtype=jnp.int32)
    earlier = (token_range[None, :] < token_range[:, None]).astype(jnp.bfloat16)
    count_before = jnp.einsum(
        "uv,bvs->bus", earlier, token_hit.astype(jnp.bfloat16), preferred_element_type=jnp.float32
    )
    rank_range = jnp.arange(capacity, dtype=jnp.float32)
    pick = token_hit[..., None] * (count_before[..., None] == rank_range)
    pick_hot = pick.astype(jnp.bfloat16)
    received = jnp.einsum(
        "busr,bud->bsrd", pick_hot, all_rows, preferred_element_type=jnp.float32
    ).astype(jnp.bfloat16).reshape(holders, groups, slot_dev, capacity, model_width)
    partial_value = expert_partial(received, expert_weights).astype(jnp.bfloat16)
    if blocks * row_count * model_width * 4 <= (32 << 20):
        partial_value = partial_value.reshape(blocks, slot_dev, capacity, model_width)
        weight_hi = (pick * gate_sel_hi[..., None]).astype(jnp.bfloat16)
        weight_lo = (pick * gate_sel_lo[..., None]).astype(jnp.bfloat16)
        weight_both = jnp.concatenate([weight_hi, weight_lo], axis=1)
        combined = jnp.einsum(
            "busr,bsrd->bud", weight_both, partial_value, preferred_element_type=jnp.float32
        )
        token_sum = (combined[:, :row_count] + combined[:, row_count:]).reshape(-1, model_width)
        moe_sum = lax.psum_scatter(
            token_sum, ("expert", "tensor"), scatter_dimension=0, tiled=True
        )
    else:
        expert_sum = lax.psum_scatter(partial_value, "tensor", scatter_dimension=1, tiled=True)
        returned = lax.all_to_all(expert_sum, "expert", split_axis=0, concat_axis=0, tiled=True)
        own_flat = own_ids.reshape(-1)
        own_onehot_flat = own_flat[:, None] == expert_range
        slot_of = jnp.sum(
            jnp.where(own_onehot_flat, slot_pick[my_holder][None, :], 0), axis=-1
        )
        slot_hot = (slot_of[:, None] == slot_range).astype(jnp.int32)
        rank_in = jnp.sum(jnp.cumsum(slot_hot, axis=0) * slot_hot, axis=-1) - 1
        own_index = slot_of * capacity + rank_in
        outputs = returned.reshape(-1, model_width)[own_index].reshape(
            row_count, top_count, model_width
        )
        moe_sum = jnp.einsum("rk,rkd->rd", gate_weights, outputs.astype(jnp.float32))
    hidden_out = hidden_mid + moe_sum
    normed_out = rms_scale(hidden_out, post_gain)
    return (hidden_out, normed_out)


def solution(mesh):
    in_specs = (
        P("expert", "tensor"),
        P("tensor", None),
        P(("expert", "tensor"), None),
        P(),
        P(),
        P("expert", None),
        P(),
        P("expert", None, None, "tensor"),
        P(),
    )
    out_specs = (P(("expert", "tensor"), None), P(("expert", "tensor"), None))
    return jax.shard_map(
        on_device, mesh=mesh, in_specs=in_specs, out_specs=out_specs, check_vma=False
    )
```

```python
import jax
import jax.numpy as jnp
from jax import lax
from jax.sharding import PartitionSpec as P

EPS = 1e-06


def rms_scale(values, gain_row):
    mean_square = jnp.mean(values * values, axis=-1, keepdims=True)
    return values * lax.rsqrt(mean_square + EPS) * gain_row


def expert_partial(block_rows, weights):
    gate_pre = jnp.einsum(
        "nqsmd,sdf->nqsmf", block_rows, weights[:, 0], preferred_element_type=jnp.float32
    )
    up_pre = jnp.einsum(
        "nqsmd,sdf->nqsmf", block_rows, weights[:, 1], preferred_element_type=jnp.float32
    )
    inner_act = (jax.nn.silu(gate_pre) * up_pre).astype(jnp.bfloat16)
    return jnp.einsum(
        "nqsmf,sdf->nqsmd", inner_act, weights[:, 2], preferred_element_type=jnp.float32
    )


def on_device(
    context,
    out_proj,
    residual,
    norm_gain,
    router_weight,
    expert_ids,
    placement,
    expert_weights,
    post_gain,
):
    groups = lax.axis_size("tensor")
    holders = lax.axis_size("expert")
    my_group = lax.axis_index("tensor")
    my_holder = lax.axis_index("expert")
    row_count = residual.shape[0]
    model_width = residual.shape[1]
    top_count = expert_ids.shape[1]
    expert_count = router_weight.shape[1]
    slot_dev = expert_weights.shape[0]
    slot_total = placement.shape[0]
    blocks = holders * groups
    capacity = max(2, row_count * top_count * 5 // (expert_count * 4))
    expert_range = jnp.arange(expert_count, dtype=jnp.int32)
    slot_range = jnp.arange(slot_total, dtype=jnp.int32)
    attention = lax.psum_scatter(
        jnp.dot(context, out_proj, preferred_element_type=jnp.float32).astype(jnp.bfloat16),
        "tensor",
        scatter_dimension=0,
        tiled=True,
    ).astype(jnp.float32)
    hidden_mid = residual.astype(jnp.float32) + attention
    normed_full = rms_scale(hidden_mid, norm_gain)
    normed = normed_full.astype(jnp.bfloat16)
    logits = jnp.dot(normed_full, router_weight, precision=lax.Precision.HIGHEST)
    own_ids = lax.dynamic_slice_in_dim(expert_ids, my_group * row_count, row_count, 0)
    own_onehot = own_ids[:, :, None] == expert_range[None, None, :]
    chosen = jnp.sum(jnp.where(own_onehot, logits[:, None, :], 0.0), axis=-1)
    gate_weights = jax.nn.softmax(chosen, axis=-1)
    gate_hi = gate_weights.astype(jnp.bfloat16)
    gate_lo = (gate_weights - gate_hi.astype(jnp.float32)).astype(jnp.bfloat16)
    side = jnp.concatenate([own_ids.astype(jnp.bfloat16), gate_hi, gate_lo], axis=1)
    side = jnp.pad(side, ((0, 0), (0, 128 - 3 * top_count)))
    packed = lax.all_gather(
        jnp.concatenate([normed, side], axis=1), ("expert", "tensor"), axis=0, tiled=True
    ).reshape(blocks, row_count, model_width + 128)
    all_rows = packed[:, :, :model_width]
    all_ids = packed[:, :, model_width:model_width + top_count].astype(jnp.int32)
    all_hi = packed[:, :, model_width + top_count:model_width + 2 * top_count]
    all_lo = packed[:, :, model_width + 2 * top_count:model_width + 3 * top_count]
    holds = (placement[None, :] == expert_range[:, None]).astype(jnp.int32)
    copies = jnp.sum(holds, axis=1)
    copy_rank = jnp.cumsum(holds, axis=1) - 1
    holder_range = jnp.arange(holders, dtype=jnp.int32)
    copy_pick = holder_range[:, None] % copies[None, :]
    picked = (holds[None] > 0) & (copy_rank[None] == copy_pick[:, :, None])
    slot_pick = jnp.sum(jnp.where(picked, slot_range[None, None, :], 0), axis=2)
    local_range = jnp.arange(slot_dev, dtype=jnp.int32)
    mine_map = (slot_pick[:, :, None] == my_holder * slot_dev + local_range).astype(jnp.bfloat16)
    block_holder = jnp.arange(blocks, dtype=jnp.int32) // groups
    block_map = mine_map[block_holder]
    names = all_ids[:, :, :, None] == expert_range
    name_hot = jnp.any(names, axis=2).astype(jnp.bfloat16)
    gate_e_hi = jnp.sum(jnp.where(names, all_hi[:, :, :, None], 0), axis=2).astype(jnp.bfloat16)
    gate_e_lo = jnp.sum(jnp.where(names, all_lo[:, :, :, None], 0), axis=2).astype(jnp.bfloat16)
    stack = jnp.concatenate([name_hot, gate_e_hi, gate_e_lo], axis=1)
    per_slot = jnp.einsum("bue,bes->bus", stack, block_map, preferred_element_type=jnp.float32)
    token_hit = per_slot[:, :row_count]
    gate_sel_hi = per_slot[:, row_count:2 * row_count]
    gate_sel_lo = per_slot[:, 2 * row_count:]
    token_range = jnp.arange(row_count, dtype=jnp.int32)
    earlier = (token_range[None, :] < token_range[:, None]).astype(jnp.bfloat16)
    count_before = jnp.einsum(
        "uv,bvs->bus", earlier, token_hit.astype(jnp.bfloat16), preferred_element_type=jnp.float32
    )
    rank_range = jnp.arange(capacity, dtype=jnp.float32)
    pick = token_hit[..., None] * (count_before[..., None] == rank_range)
    pick_hot = pick.astype(jnp.bfloat16)
    received = jnp.einsum(
        "busr,bud->bsrd", pick_hot, all_rows, preferred_element_type=jnp.float32
    ).astype(jnp.bfloat16).reshape(holders, groups, slot_dev, capacity, model_width)
    partial_value = expert_partial(received, expert_weights).astype(jnp.bfloat16)
    if blocks * row_count * model_width * 4 <= (32 << 20):
        partial_value = partial_value.reshape(blocks, slot_dev, capacity, model_width)
        weight_hi = (pick * gate_sel_hi[..., None]).astype(jnp.bfloat16)
        weight_lo = (pick * gate_sel_lo[..., None]).astype(jnp.bfloat16)
        combined = jnp.einsum(
            "busr,bsrd->bud", weight_hi, partial_value, preferred_element_type=jnp.float32
        ) + jnp.einsum(
            "busr,bsrd->bud", weight_lo, partial_value, preferred_element_type=jnp.float32
        )
        token_sum = combined.astype(jnp.bfloat16).reshape(-1, model_width)
        moe_sum = lax.psum_scatter(
            token_sum, ("expert", "tensor"), scatter_dimension=0, tiled=True
        ).astype(jnp.float32)
    else:
        expert_sum = lax.psum_scatter(partial_value, "tensor", scatter_dimension=1, tiled=True)
        returned = lax.all_to_all(expert_sum, "expert", split_axis=0, concat_axis=0, tiled=True)
        own_flat = own_ids.reshape(-1)
        own_onehot_flat = own_flat[:, None] == expert_range
        slot_of = jnp.sum(
            jnp.where(own_onehot_flat, slot_pick[my_holder][None, :], 0), axis=-1
        )
        slot_hot = (slot_of[:, None] == slot_range).astype(jnp.int32)
        rank_in = jnp.sum(jnp.cumsum(slot_hot, axis=0) * slot_hot, axis=-1) - 1
        own_index = slot_of * capacity + rank_in
        outputs = returned.reshape(-1, model_width)[own_index].reshape(
            row_count, top_count, model_width
        )
        moe_sum = jnp.einsum("rk,rkd->rd", gate_weights, outputs.astype(jnp.float32))
    hidden_out = hidden_mid + moe_sum
    normed_out = rms_scale(hidden_out, post_gain)
    return (hidden_out, normed_out)


def solution(mesh):
    in_specs = (
        P("expert", "tensor"),
        P("tensor", None),
        P(("expert", "tensor"), None),
        P(),
        P(),
        P("expert", None),
        P(),
        P("expert", None, None, "tensor"),
        P(),
    )
    out_specs = (P(("expert", "tensor"), None), P(("expert", "tensor"), None))
    return jax.shard_map(
        on_device, mesh=mesh, in_specs=in_specs, out_specs=out_specs, check_vma=False
    )
```

```python
import jax
import jax.numpy as jnp
from jax import lax
from jax.sharding import PartitionSpec as P

EPS = 1e-06


def rms_scale(values, gain_row):
    mean_square = jnp.mean(values * values, axis=-1, keepdims=True)
    return values * lax.rsqrt(mean_square + EPS) * gain_row


def expert_partial(block_rows, weights):
    gate_pre = jnp.einsum(
        "nqsmd,sdf->nqsmf", block_rows, weights[:, 0], preferred_element_type=jnp.float32
    )
    up_pre = jnp.einsum(
        "nqsmd,sdf->nqsmf", block_rows, weights[:, 1], preferred_element_type=jnp.float32
    )
    inner_act = (jax.nn.silu(gate_pre) * up_pre).astype(jnp.bfloat16)
    return jnp.einsum(
        "nqsmf,sdf->nqsmd", inner_act, weights[:, 2], preferred_element_type=jnp.float32
    )


def on_device(
    context,
    out_proj,
    residual,
    norm_gain,
    router_weight,
    expert_ids,
    placement,
    expert_weights,
    post_gain,
):
    groups = lax.axis_size("tensor")
    holders = lax.axis_size("expert")
    my_group = lax.axis_index("tensor")
    my_holder = lax.axis_index("expert")
    row_count = residual.shape[0]
    model_width = residual.shape[1]
    top_count = expert_ids.shape[1]
    expert_count = router_weight.shape[1]
    slot_dev = expert_weights.shape[0]
    slot_total = placement.shape[0]
    blocks = holders * groups
    capacity = max(2, row_count * top_count * 5 // (expert_count * 4))
    expert_range = jnp.arange(expert_count, dtype=jnp.int32)
    slot_range = jnp.arange(slot_total, dtype=jnp.int32)
    attention = lax.psum_scatter(
        jnp.dot(context, out_proj, preferred_element_type=jnp.float32).astype(jnp.bfloat16),
        "tensor",
        scatter_dimension=0,
        tiled=True,
    ).astype(jnp.float32)
    hidden_mid = residual.astype(jnp.float32) + attention
    normed_full = rms_scale(hidden_mid, norm_gain)
    normed = normed_full.astype(jnp.bfloat16)
    logits = jnp.dot(normed_full, router_weight, precision=lax.Precision.HIGHEST)
    own_ids = lax.dynamic_slice_in_dim(expert_ids, my_group * row_count, row_count, 0)
    own_onehot = own_ids[:, :, None] == expert_range[None, None, :]
    chosen = jnp.sum(jnp.where(own_onehot, logits[:, None, :], 0.0), axis=-1)
    gate_weights = jax.nn.softmax(chosen, axis=-1)
    gate_hi = gate_weights.astype(jnp.bfloat16)
    gate_lo = (gate_weights - gate_hi.astype(jnp.float32)).astype(jnp.bfloat16)
    side = jnp.concatenate([own_ids.astype(jnp.bfloat16), gate_hi, gate_lo], axis=1)
    side = jnp.pad(side, ((0, 0), (0, 128 - 3 * top_count)))
    packed = lax.all_gather(
        jnp.concatenate([normed, side], axis=1), ("expert", "tensor"), axis=0, tiled=True
    ).reshape(blocks, row_count, model_width + 128)
    all_rows = packed[:, :, :model_width]
    all_ids = packed[:, :, model_width:model_width + top_count].astype(jnp.int32)
    all_hi = packed[:, :, model_width + top_count:model_width + 2 * top_count]
    all_lo = packed[:, :, model_width + 2 * top_count:model_width + 3 * top_count]
    holds = (placement[None, :] == expert_range[:, None]).astype(jnp.int32)
    copies = jnp.sum(holds, axis=1)
    copy_rank = jnp.cumsum(holds, axis=1) - 1
    holder_range = jnp.arange(holders, dtype=jnp.int32)
    copy_pick = holder_range[:, None] % copies[None, :]
    picked = (holds[None] > 0) & (copy_rank[None] == copy_pick[:, :, None])
    slot_pick = jnp.sum(jnp.where(picked, slot_range[None, None, :], 0), axis=2)
    local_range = jnp.arange(slot_dev, dtype=jnp.int32)
    mine_map = (slot_pick[:, :, None] == my_holder * slot_dev + local_range).astype(jnp.bfloat16)
    block_holder = jnp.arange(blocks, dtype=jnp.int32) // groups
    block_map = mine_map[block_holder]
    names = all_ids[:, :, :, None] == expert_range
    name_hot = jnp.any(names, axis=2).astype(jnp.bfloat16)
    gate_e_hi = jnp.sum(jnp.where(names, all_hi[:, :, :, None], 0), axis=2).astype(jnp.bfloat16)
    gate_e_lo = jnp.sum(jnp.where(names, all_lo[:, :, :, None], 0), axis=2).astype(jnp.bfloat16)
    stack = jnp.concatenate([name_hot, gate_e_hi, gate_e_lo], axis=1)
    per_slot = jnp.einsum("bue,bes->bus", stack, block_map, preferred_element_type=jnp.float32)
    token_hit = per_slot[:, :row_count]
    gate_sel_hi = per_slot[:, row_count:2 * row_count]
    gate_sel_lo = per_slot[:, 2 * row_count:]
    token_range = jnp.arange(row_count, dtype=jnp.int32)
    earlier = (token_range[None, :] < token_range[:, None]).astype(jnp.bfloat16)
    count_before = jnp.einsum(
        "uv,bvs->bus", earlier, token_hit.astype(jnp.bfloat16), preferred_element_type=jnp.float32
    )
    rank_range = jnp.arange(capacity, dtype=jnp.float32)
    pick = token_hit[..., None] * (count_before[..., None] == rank_range)
    pick_hot = pick.astype(jnp.bfloat16)
    received = jnp.einsum(
        "busr,bud->bsrd", pick_hot, all_rows, preferred_element_type=jnp.float32
    ).astype(jnp.bfloat16).reshape(holders, groups, slot_dev, capacity, model_width)
    partial_value = expert_partial(received, expert_weights).astype(jnp.bfloat16)
    if blocks * row_count * model_width * 4 <= (32 << 20):
        partial_value = partial_value.reshape(blocks, slot_dev, capacity, model_width)
        weight_hi = (pick * gate_sel_hi[..., None]).astype(jnp.bfloat16)
        weight_lo = (pick * gate_sel_lo[..., None]).astype(jnp.bfloat16)
        combined = jnp.einsum(
            "busr,bsrd->bud", weight_hi, partial_value, preferred_element_type=jnp.float32
        ) + jnp.einsum(
            "busr,bsrd->bud", weight_lo, partial_value, preferred_element_type=jnp.float32
        )
        token_sum = combined.reshape(holders, groups * row_count, model_width)
        moe_sum = lax.psum_scatter(token_sum, "expert", scatter_dimension=0, tiled=False)
        moe_sum = lax.psum_scatter(moe_sum, "tensor", scatter_dimension=0, tiled=True)
    else:
        expert_sum = lax.psum_scatter(partial_value, "tensor", scatter_dimension=1, tiled=True)
        returned = lax.all_to_all(expert_sum, "expert", split_axis=0, concat_axis=0, tiled=True)
        own_flat = own_ids.reshape(-1)
        own_onehot_flat = own_flat[:, None] == expert_range
        slot_of = jnp.sum(
            jnp.where(own_onehot_flat, slot_pick[my_holder][None, :], 0), axis=-1
        )
        slot_hot = (slot_of[:, None] == slot_range).astype(jnp.int32)
        rank_in = jnp.sum(jnp.cumsum(slot_hot, axis=0) * slot_hot, axis=-1) - 1
        own_index = slot_of * capacity + rank_in
        outputs = returned.reshape(-1, model_width)[own_index].reshape(
            row_count, top_count, model_width
        )
        moe_sum = jnp.einsum("rk,rkd->rd", gate_weights, outputs.astype(jnp.float32))
    hidden_out = hidden_mid + moe_sum
    normed_out = rms_scale(hidden_out, post_gain)
    return (hidden_out, normed_out)


def solution(mesh):
    in_specs = (
        P("expert", "tensor"),
        P("tensor", None),
        P(("expert", "tensor"), None),
        P(),
        P(),
        P("expert", None),
        P(),
        P("expert", None, None, "tensor"),
        P(),
    )
    out_specs = (P(("expert", "tensor"), None), P(("expert", "tensor"), None))
    return jax.shard_map(
        on_device, mesh=mesh, in_specs=in_specs, out_specs=out_specs, check_vma=False
    )
```

```python
import jax
import jax.numpy as jnp
from jax import lax
from jax.sharding import PartitionSpec as P

EPS = 1e-06


def rms_scale(values, gain_row):
    mean_square = jnp.mean(values * values, axis=-1, keepdims=True)
    return values * lax.rsqrt(mean_square + EPS) * gain_row


def expert_inner(block_rows, weights):
    both_pre = jnp.einsum(
        "nqsmd,scdf->nqsmcf", block_rows, weights[:, :2], preferred_element_type=jnp.float32
    )
    return jax.nn.silu(both_pre[..., 0, :]) * both_pre[..., 1, :]


def expert_down(inner_act, weights):
    return jnp.einsum(
        "nqsmf,sdf->nqsmd", inner_act, weights[:, 2], preferred_element_type=jnp.float32
    )


def on_device(
    context,
    out_proj,
    residual,
    norm_gain,
    router_weight,
    expert_ids,
    placement,
    expert_weights,
    post_gain,
):
    groups = lax.axis_size("tensor")
    holders = lax.axis_size("expert")
    my_group = lax.axis_index("tensor")
    my_holder = lax.axis_index("expert")
    row_count = residual.shape[0]
    model_width = residual.shape[1]
    top_count = expert_ids.shape[1]
    expert_count = router_weight.shape[1]
    slot_dev = expert_weights.shape[0]
    slot_total = placement.shape[0]
    blocks = holders * groups
    capacity = max(2, row_count * top_count * 5 // (expert_count * 4))
    expert_range = jnp.arange(expert_count, dtype=jnp.int32)
    slot_range = jnp.arange(slot_total, dtype=jnp.int32)
    attention = lax.psum_scatter(
        jnp.dot(context, out_proj, preferred_element_type=jnp.float32).astype(jnp.bfloat16),
        "tensor",
        scatter_dimension=0,
        tiled=True,
    ).astype(jnp.float32)
    hidden_mid = residual.astype(jnp.float32) + attention
    normed_full = rms_scale(hidden_mid, norm_gain)
    normed = normed_full.astype(jnp.bfloat16)
    logits = jnp.dot(normed_full, router_weight, precision=lax.Precision.HIGHEST)
    own_ids = lax.dynamic_slice_in_dim(expert_ids, my_group * row_count, row_count, 0)
    own_onehot = own_ids[:, :, None] == expert_range[None, None, :]
    chosen = jnp.sum(jnp.where(own_onehot, logits[:, None, :], 0.0), axis=-1)
    gate_weights = jax.nn.softmax(chosen, axis=-1)
    gate_hi = gate_weights.astype(jnp.bfloat16)
    gate_lo = (gate_weights - gate_hi.astype(jnp.float32)).astype(jnp.bfloat16)
    side = jnp.concatenate([own_ids.astype(jnp.bfloat16), gate_hi, gate_lo], axis=1)
    side = jnp.pad(side, ((0, 0), (0, 128 - 3 * top_count)))
    packed = lax.all_gather(
        jnp.concatenate([normed, side], axis=1), ("expert", "tensor"), axis=0, tiled=True
    ).reshape(blocks, row_count, model_width + 128)
    all_rows = packed[:, :, :model_width]
    all_ids = packed[:, :, model_width:model_width + top_count].astype(jnp.int32)
    all_hi = packed[:, :, model_width + top_count:model_width + 2 * top_count]
    all_lo = packed[:, :, model_width + 2 * top_count:model_width + 3 * top_count]
    holds = (placement[None, :] == expert_range[:, None]).astype(jnp.int32)
    copies = jnp.sum(holds, axis=1)
    copy_rank = jnp.cumsum(holds, axis=1) - 1
    holder_range = jnp.arange(holders, dtype=jnp.int32)
    copy_pick = holder_range[:, None] % copies[None, :]
    picked = (holds[None] > 0) & (copy_rank[None] == copy_pick[:, :, None])
    slot_pick = jnp.sum(jnp.where(picked, slot_range[None, None, :], 0), axis=2)
    local_range = jnp.arange(slot_dev, dtype=jnp.int32)
    mine_map = (slot_pick[:, :, None] == my_holder * slot_dev + local_range).astype(jnp.bfloat16)
    block_holder = jnp.arange(blocks, dtype=jnp.int32) // groups
    block_map = mine_map[block_holder]
    names = all_ids[:, :, :, None] == expert_range
    name_hot = jnp.any(names, axis=2).astype(jnp.bfloat16)
    gate_e_hi = jnp.sum(jnp.where(names, all_hi[:, :, :, None], 0), axis=2).astype(jnp.bfloat16)
    gate_e_lo = jnp.sum(jnp.where(names, all_lo[:, :, :, None], 0), axis=2).astype(jnp.bfloat16)
    stack = jnp.concatenate([name_hot, gate_e_hi, gate_e_lo], axis=1)
    per_slot = jnp.einsum("bue,bes->bus", stack, block_map, preferred_element_type=jnp.float32)
    token_hit = per_slot[:, :row_count]
    gate_sel_hi = per_slot[:, row_count:2 * row_count]
    gate_sel_lo = per_slot[:, 2 * row_count:]
    token_range = jnp.arange(row_count, dtype=jnp.int32)
    earlier = (token_range[None, :] < token_range[:, None]).astype(jnp.bfloat16)
    count_before = jnp.einsum(
        "uv,bvs->bus", earlier, token_hit.astype(jnp.bfloat16), preferred_element_type=jnp.float32
    )
    rank_range = jnp.arange(capacity, dtype=jnp.float32)
    pick = token_hit[..., None] * (count_before[..., None] == rank_range)
    pick_hot = pick.astype(jnp.bfloat16)
    received = jnp.einsum(
        "busr,bud->bsrd", pick_hot, all_rows, preferred_element_type=jnp.float32
    ).astype(jnp.bfloat16).reshape(holders, groups, slot_dev, capacity, model_width)
    inner_f32 = expert_inner(received, expert_weights)
    if blocks * row_count * model_width * 4 <= (32 << 20):
        gate_sel = gate_sel_hi + gate_sel_lo
        pair_gate = jnp.sum(pick * gate_sel[..., None], axis=1)
        pair_gate = pair_gate.reshape(holders, groups, slot_dev, capacity, 1)
        inner_act = (inner_f32 * pair_gate).astype(jnp.bfloat16)
        partial_value = expert_down(inner_act, expert_weights).astype(jnp.bfloat16)
        partial_value = partial_value.reshape(blocks, slot_dev, capacity, model_width)
        combined = jnp.einsum(
            "busr,bsrd->bud", pick_hot, partial_value, preferred_element_type=jnp.float32
        )
        token_sum = combined.astype(jnp.bfloat16).reshape(-1, model_width)
        moe_sum = lax.psum_scatter(
            token_sum, ("expert", "tensor"), scatter_dimension=0, tiled=True
        ).astype(jnp.float32)
    else:
        partial_value = expert_down(
            inner_f32.astype(jnp.bfloat16), expert_weights
        ).astype(jnp.bfloat16)
        expert_sum = lax.psum_scatter(partial_value, "tensor", scatter_dimension=1, tiled=True)
        returned = lax.all_to_all(expert_sum, "expert", split_axis=0, concat_axis=0, tiled=True)
        own_flat = own_ids.reshape(-1)
        own_onehot_flat = own_flat[:, None] == expert_range
        slot_of = jnp.sum(
            jnp.where(own_onehot_flat, slot_pick[my_holder][None, :], 0), axis=-1
        )
        slot_hot = (slot_of[:, None] == slot_range).astype(jnp.int32)
        rank_in = jnp.sum(jnp.cumsum(slot_hot, axis=0) * slot_hot, axis=-1) - 1
        own_index = slot_of * capacity + rank_in
        outputs = returned.reshape(-1, model_width)[own_index].reshape(
            row_count, top_count, model_width
        )
        moe_sum = jnp.einsum("rk,rkd->rd", gate_weights, outputs.astype(jnp.float32))
    hidden_out = hidden_mid + moe_sum
    normed_out = rms_scale(hidden_out, post_gain)
    return (hidden_out, normed_out)


def solution(mesh):
    in_specs = (
        P("expert", "tensor"),
        P("tensor", None),
        P(("expert", "tensor"), None),
        P(),
        P(),
        P("expert", None),
        P(),
        P("expert", None, None, "tensor"),
        P(),
    )
    out_specs = (P(("expert", "tensor"), None), P(("expert", "tensor"), None))
    return jax.shard_map(
        on_device, mesh=mesh, in_specs=in_specs, out_specs=out_specs, check_vma=False
    )
```

```python
import jax
import jax.numpy as jnp
from jax import lax
from jax.sharding import PartitionSpec as P

EPS = 1e-06


def rms_scale(values, gain_row):
    mean_square = jnp.mean(values * values, axis=-1, keepdims=True)
    return values * lax.rsqrt(mean_square + EPS) * gain_row


def expert_inner(block_rows, weights):
    both_pre = jnp.einsum(
        "nqsmd,scdf->nqsmcf", block_rows, weights[:, :2], preferred_element_type=jnp.float32
    )
    return jax.nn.silu(both_pre[..., 0, :]) * both_pre[..., 1, :]


def expert_down(inner_act, weights):
    return jnp.einsum(
        "nqsmf,sdf->nqsmd", inner_act, weights[:, 2], preferred_element_type=jnp.float32
    )


def on_device(
    context,
    out_proj,
    residual,
    norm_gain,
    router_weight,
    expert_ids,
    placement,
    expert_weights,
    post_gain,
):
    groups = lax.axis_size("tensor")
    holders = lax.axis_size("expert")
    my_group = lax.axis_index("tensor")
    my_holder = lax.axis_index("expert")
    row_count = residual.shape[0]
    model_width = residual.shape[1]
    top_count = expert_ids.shape[1]
    expert_count = router_weight.shape[1]
    slot_dev = expert_weights.shape[0]
    slot_total = placement.shape[0]
    blocks = holders * groups
    capacity = max(2, row_count * top_count * 5 // (expert_count * 4))
    expert_range = jnp.arange(expert_count, dtype=jnp.int32)
    slot_range = jnp.arange(slot_total, dtype=jnp.int32)
    attention = lax.psum_scatter(
        jnp.dot(context, out_proj, preferred_element_type=jnp.float32).astype(jnp.bfloat16),
        "tensor",
        scatter_dimension=0,
        tiled=True,
    ).astype(jnp.float32)
    hidden_mid = residual.astype(jnp.float32) + attention
    normed_full = rms_scale(hidden_mid, norm_gain)
    normed = normed_full.astype(jnp.bfloat16)
    logits = jnp.dot(normed_full, router_weight, precision=lax.Precision.HIGHEST)
    own_ids = lax.dynamic_slice_in_dim(expert_ids, my_group * row_count, row_count, 0)
    own_onehot = own_ids[:, :, None] == expert_range[None, None, :]
    chosen = jnp.sum(jnp.where(own_onehot, logits[:, None, :], 0.0), axis=-1)
    gate_weights = jax.nn.softmax(chosen, axis=-1)
    gate_hi = gate_weights.astype(jnp.bfloat16)
    gate_lo = (gate_weights - gate_hi.astype(jnp.float32)).astype(jnp.bfloat16)
    side = jnp.concatenate([own_ids.astype(jnp.bfloat16), gate_hi, gate_lo], axis=1)
    side = jnp.pad(side, ((0, 0), (0, 128 - 3 * top_count)))
    packed = lax.all_gather(
        jnp.concatenate([normed, side], axis=1), ("expert", "tensor"), axis=0, tiled=True
    ).reshape(blocks, row_count, model_width + 128)
    all_rows = packed[:, :, :model_width]
    all_ids = packed[:, :, model_width:model_width + top_count].astype(jnp.int32)
    all_hi = packed[:, :, model_width + top_count:model_width + 2 * top_count]
    all_lo = packed[:, :, model_width + 2 * top_count:model_width + 3 * top_count]
    holds = (placement[None, :] == expert_range[:, None]).astype(jnp.int32)
    copies = jnp.sum(holds, axis=1)
    copy_rank = jnp.cumsum(holds, axis=1) - 1
    holder_range = jnp.arange(holders, dtype=jnp.int32)
    copy_pick = holder_range[:, None] % copies[None, :]
    picked = (holds[None] > 0) & (copy_rank[None] == copy_pick[:, :, None])
    slot_pick = jnp.sum(jnp.where(picked, slot_range[None, None, :], 0), axis=2)
    local_range = jnp.arange(slot_dev, dtype=jnp.int32)
    mine_map = (slot_pick[:, :, None] == my_holder * slot_dev + local_range).astype(jnp.bfloat16)
    block_holder = jnp.arange(blocks, dtype=jnp.int32) // groups
    block_map = mine_map[block_holder]
    names = all_ids[:, :, :, None] == expert_range
    name_hot = jnp.any(names, axis=2).astype(jnp.bfloat16)
    gate_e_hi = jnp.sum(jnp.where(names, all_hi[:, :, :, None], 0), axis=2).astype(jnp.bfloat16)
    gate_e_lo = jnp.sum(jnp.where(names, all_lo[:, :, :, None], 0), axis=2).astype(jnp.bfloat16)
    stack = jnp.concatenate([name_hot, gate_e_hi, gate_e_lo], axis=1)
    per_slot = jnp.einsum("bue,bes->bus", stack, block_map, preferred_element_type=jnp.float32)
    token_hit = per_slot[:, :row_count]
    gate_sel_hi = per_slot[:, row_count:2 * row_count]
    gate_sel_lo = per_slot[:, 2 * row_count:]
    token_range = jnp.arange(row_count, dtype=jnp.int32)
    earlier = (token_range[None, :] < token_range[:, None]).astype(jnp.bfloat16)
    count_before = jnp.einsum(
        "uv,bvs->bus", earlier, token_hit.astype(jnp.bfloat16), preferred_element_type=jnp.float32
    )
    rank_range = jnp.arange(capacity, dtype=jnp.float32)
    pick = token_hit[..., None] * (count_before[..., None] == rank_range)
    pick_hot = pick.astype(jnp.bfloat16)
    received = jnp.einsum(
        "busr,bud->bsrd", pick_hot, all_rows, preferred_element_type=jnp.float32
    ).astype(jnp.bfloat16).reshape(holders, groups, slot_dev, capacity, model_width)
    inner_f32 = expert_inner(received, expert_weights)
    if blocks * row_count * model_width * 4 <= (32 << 20):
        gate_sel = gate_sel_hi + gate_sel_lo
        pair_gate = jnp.sum(pick * gate_sel[..., None], axis=1)
        pair_gate = pair_gate.reshape(holders, groups, slot_dev, capacity, 1)
        inner_act = (inner_f32 * pair_gate).astype(jnp.bfloat16)
        partial_value = expert_down(inner_act, expert_weights).astype(jnp.bfloat16)
        partial_value = partial_value.reshape(blocks, slot_dev, capacity, model_width)
        combined = jnp.einsum(
            "busr,bsrd->bud", pick_hot, partial_value, preferred_element_type=jnp.float32
        )
        token_sum = combined.astype(jnp.bfloat16).reshape(holders, groups, row_count, model_width)
        moe_sum = lax.psum_scatter(token_sum, "tensor", scatter_dimension=1, tiled=False)
        moe_sum = lax.psum_scatter(
            moe_sum, "expert", scatter_dimension=0, tiled=False
        ).astype(jnp.float32)
    else:
        partial_value = expert_down(
            inner_f32.astype(jnp.bfloat16), expert_weights
        ).astype(jnp.bfloat16)
        expert_sum = lax.psum_scatter(partial_value, "tensor", scatter_dimension=1, tiled=True)
        returned = lax.all_to_all(expert_sum, "expert", split_axis=0, concat_axis=0, tiled=True)
        own_flat = own_ids.reshape(-1)
        own_onehot_flat = own_flat[:, None] == expert_range
        slot_of = jnp.sum(
            jnp.where(own_onehot_flat, slot_pick[my_holder][None, :], 0), axis=-1
        )
        slot_hot = (slot_of[:, None] == slot_range).astype(jnp.int32)
        rank_in = jnp.sum(jnp.cumsum(slot_hot, axis=0) * slot_hot, axis=-1) - 1
        own_index = slot_of * capacity + rank_in
        outputs = returned.reshape(-1, model_width)[own_index].reshape(
            row_count, top_count, model_width
        )
        moe_sum = jnp.einsum("rk,rkd->rd", gate_weights, outputs.astype(jnp.float32))
    hidden_out = hidden_mid + moe_sum
    normed_out = rms_scale(hidden_out, post_gain)
    return (hidden_out, normed_out)


def solution(mesh):
    in_specs = (
        P("expert", "tensor"),
        P("tensor", None),
        P(("expert", "tensor"), None),
        P(),
        P(),
        P("expert", None),
        P(),
        P("expert", None, None, "tensor"),
        P(),
    )
    out_specs = (P(("expert", "tensor"), None), P(("expert", "tensor"), None))
    return jax.shard_map(
        on_device, mesh=mesh, in_specs=in_specs, out_specs=out_specs, check_vma=False
    )
```

```python
import jax
import jax.numpy as jnp
from jax import lax
from jax.sharding import PartitionSpec as P

EPS = 1e-06


def rms_scale(values, gain_row):
    mean_square = jnp.mean(values * values, axis=-1, keepdims=True)
    return values * lax.rsqrt(mean_square + EPS) * gain_row


def expert_inner(block_rows, weights):
    both_pre = jnp.einsum(
        "nqsmd,scdf->nqsmcf", block_rows, weights[:, :2], preferred_element_type=jnp.float32
    )
    return jax.nn.silu(both_pre[..., 0, :]) * both_pre[..., 1, :]


def expert_down(inner_act, weights):
    return jnp.einsum(
        "nqsmf,sdf->nqsmd", inner_act, weights[:, 2], preferred_element_type=jnp.float32
    )


def on_device(
    context,
    out_proj,
    residual,
    norm_gain,
    router_weight,
    expert_ids,
    placement,
    expert_weights,
    post_gain,
):
    groups = lax.axis_size("tensor")
    holders = lax.axis_size("expert")
    my_group = lax.axis_index("tensor")
    my_holder = lax.axis_index("expert")
    row_count = residual.shape[0]
    model_width = residual.shape[1]
    top_count = expert_ids.shape[1]
    expert_count = router_weight.shape[1]
    slot_dev = expert_weights.shape[0]
    slot_total = placement.shape[0]
    blocks = holders * groups
    capacity = max(2, row_count * top_count * 5 // (expert_count * 4))
    expert_range = jnp.arange(expert_count, dtype=jnp.int32)
    slot_range = jnp.arange(slot_total, dtype=jnp.int32)
    attention = lax.psum_scatter(
        jnp.dot(context, out_proj, preferred_element_type=jnp.float32).astype(jnp.bfloat16),
        "tensor",
        scatter_dimension=0,
        tiled=True,
    ).astype(jnp.float32)
    hidden_mid = residual.astype(jnp.float32) + attention
    normed_full = rms_scale(hidden_mid, norm_gain)
    normed = normed_full.astype(jnp.bfloat16)
    logits = jnp.dot(normed_full, router_weight, precision=lax.Precision.HIGHEST)
    own_ids = lax.dynamic_slice_in_dim(expert_ids, my_group * row_count, row_count, 0)
    own_onehot = own_ids[:, :, None] == expert_range[None, None, :]
    chosen = jnp.sum(jnp.where(own_onehot, logits[:, None, :], 0.0), axis=-1)
    gate_weights = jax.nn.softmax(chosen, axis=-1)
    gate_hi = gate_weights.astype(jnp.bfloat16)
    gate_lo = (gate_weights - gate_hi.astype(jnp.float32)).astype(jnp.bfloat16)
    side = jnp.concatenate([own_ids.astype(jnp.bfloat16), gate_hi, gate_lo], axis=1)
    side = jnp.pad(side, ((0, 0), (0, 128 - 3 * top_count)))
    packed = lax.all_gather(
        jnp.concatenate([normed, side], axis=1), ("expert", "tensor"), axis=0, tiled=True
    ).reshape(blocks, row_count, model_width + 128)
    all_rows = packed[:, :, :model_width]
    all_ids = packed[:, :, model_width:model_width + top_count].astype(jnp.int32)
    all_hi = packed[:, :, model_width + top_count:model_width + 2 * top_count]
    all_lo = packed[:, :, model_width + 2 * top_count:model_width + 3 * top_count]
    holds = (placement[None, :] == expert_range[:, None]).astype(jnp.int32)
    copies = jnp.sum(holds, axis=1)
    copy_rank = jnp.cumsum(holds, axis=1) - 1
    holder_range = jnp.arange(holders, dtype=jnp.int32)
    copy_pick = holder_range[:, None] % copies[None, :]
    picked = (holds[None] > 0) & (copy_rank[None] == copy_pick[:, :, None])
    slot_pick = jnp.sum(jnp.where(picked, slot_range[None, None, :], 0), axis=2)
    local_range = jnp.arange(slot_dev, dtype=jnp.int32)
    mine_map = (slot_pick[:, :, None] == my_holder * slot_dev + local_range).astype(jnp.bfloat16)
    block_holder = jnp.arange(blocks, dtype=jnp.int32) // groups
    block_map = mine_map[block_holder]
    names = all_ids[:, :, :, None] == expert_range
    name_hot = jnp.any(names, axis=2).astype(jnp.bfloat16)
    gate_e_hi = jnp.sum(jnp.where(names, all_hi[:, :, :, None], 0), axis=2).astype(jnp.bfloat16)
    gate_e_lo = jnp.sum(jnp.where(names, all_lo[:, :, :, None], 0), axis=2).astype(jnp.bfloat16)
    stack = jnp.concatenate([name_hot, gate_e_hi, gate_e_lo], axis=1)
    per_slot = jnp.einsum("bue,bes->bus", stack, block_map, preferred_element_type=jnp.float32)
    token_hit = per_slot[:, :row_count]
    gate_sel_hi = per_slot[:, row_count:2 * row_count]
    gate_sel_lo = per_slot[:, 2 * row_count:]
    token_range = jnp.arange(row_count, dtype=jnp.int32)
    earlier = (token_range[None, :] < token_range[:, None]).astype(jnp.bfloat16)
    count_before = jnp.einsum(
        "uv,bvs->bus", earlier, token_hit.astype(jnp.bfloat16), preferred_element_type=jnp.float32
    )
    rank_range = jnp.arange(capacity, dtype=jnp.float32)
    pick = token_hit[..., None] * (count_before[..., None] == rank_range)
    pick_hot = pick.astype(jnp.bfloat16)
    received = jnp.einsum(
        "busr,bud->bsrd", pick_hot, all_rows, preferred_element_type=jnp.float32
    ).astype(jnp.bfloat16).reshape(holders, groups, slot_dev, capacity, model_width)
    inner_f32 = expert_inner(received, expert_weights)
    if blocks * row_count * model_width * 4 <= (32 << 20):
        gate_sel = gate_sel_hi + gate_sel_lo
        pair_gate = jnp.sum(pick * gate_sel[..., None], axis=1)
        pair_gate = pair_gate.reshape(holders, groups, slot_dev, capacity, 1)
        inner_act = (inner_f32 * pair_gate).astype(jnp.bfloat16)
        partial_value = expert_down(inner_act, expert_weights).astype(jnp.bfloat16)
        partial_value = partial_value.reshape(blocks, slot_dev, capacity, model_width)
        combined = jnp.einsum(
            "busr,bsrd->bud", pick_hot, partial_value, preferred_element_type=jnp.float32
        )
        token_sum = combined.astype(jnp.bfloat16).reshape(holders, groups, row_count, model_width)
        moe_sum = lax.psum_scatter(
            jnp.swapaxes(token_sum, 0, 1).reshape(-1, model_width),
            "tensor",
            scatter_dimension=0,
            tiled=True,
        ).reshape(holders, row_count, model_width)
        moe_sum = lax.all_to_all(moe_sum, "expert", split_axis=0, concat_axis=0, tiled=True)
        moe_sum = jnp.sum(moe_sum.astype(jnp.float32), axis=0)
    else:
        partial_value = expert_down(
            inner_f32.astype(jnp.bfloat16), expert_weights
        ).astype(jnp.bfloat16)
        expert_sum = lax.psum_scatter(partial_value, "tensor", scatter_dimension=1, tiled=True)
        returned = lax.all_to_all(expert_sum, "expert", split_axis=0, concat_axis=0, tiled=True)
        own_flat = own_ids.reshape(-1)
        own_onehot_flat = own_flat[:, None] == expert_range
        slot_of = jnp.sum(
            jnp.where(own_onehot_flat, slot_pick[my_holder][None, :], 0), axis=-1
        )
        slot_hot = (slot_of[:, None] == slot_range).astype(jnp.int32)
        rank_in = jnp.sum(jnp.cumsum(slot_hot, axis=0) * slot_hot, axis=-1) - 1
        own_index = slot_of * capacity + rank_in
        outputs = returned.reshape(-1, model_width)[own_index].reshape(
            row_count, top_count, model_width
        )
        moe_sum = jnp.einsum("rk,rkd->rd", gate_weights, outputs.astype(jnp.float32))
    hidden_out = hidden_mid + moe_sum
    normed_out = rms_scale(hidden_out, post_gain)
    return (hidden_out, normed_out)


def solution(mesh):
    in_specs = (
        P("expert", "tensor"),
        P("tensor", None),
        P(("expert", "tensor"), None),
        P(),
        P(),
        P("expert", None),
        P(),
        P("expert", None, None, "tensor"),
        P(),
    )
    out_specs = (P(("expert", "tensor"), None), P(("expert", "tensor"), None))
    return jax.shard_map(
        on_device, mesh=mesh, in_specs=in_specs, out_specs=out_specs, check_vma=False
    )
```

```python
import jax
import jax.numpy as jnp
from jax import lax
from jax.sharding import PartitionSpec as P

EPS = 1e-06


def rms_scale(values, gain_row):
    mean_square = jnp.mean(values * values, axis=-1, keepdims=True)
    return values * lax.rsqrt(mean_square + EPS) * gain_row


def expert_inner(block_rows, weights):
    both_pre = jnp.einsum(
        "sbmd,scdf->sbmcf", block_rows, weights[:, :2], preferred_element_type=jnp.float32
    )
    return jax.nn.silu(both_pre[..., 0, :]) * both_pre[..., 1, :]


def expert_down(inner_act, weights):
    return jnp.einsum(
        "sbmf,sdf->sbmd", inner_act, weights[:, 2], preferred_element_type=jnp.float32
    )


def on_device(
    context,
    out_proj,
    residual,
    norm_gain,
    router_weight,
    expert_ids,
    placement,
    expert_weights,
    post_gain,
):
    groups = lax.axis_size("tensor")
    holders = lax.axis_size("expert")
    my_group = lax.axis_index("tensor")
    my_holder = lax.axis_index("expert")
    row_count = residual.shape[0]
    model_width = residual.shape[1]
    top_count = expert_ids.shape[1]
    expert_count = router_weight.shape[1]
    slot_dev = expert_weights.shape[0]
    slot_total = placement.shape[0]
    blocks = holders * groups
    capacity = max(2, row_count * top_count * 5 // (expert_count * 4))
    expert_range = jnp.arange(expert_count, dtype=jnp.int32)
    slot_range = jnp.arange(slot_total, dtype=jnp.int32)
    attention = lax.psum_scatter(
        jnp.dot(context, out_proj, preferred_element_type=jnp.float32).astype(jnp.bfloat16),
        "tensor",
        scatter_dimension=0,
        tiled=True,
    ).astype(jnp.float32)
    hidden_mid = residual.astype(jnp.float32) + attention
    normed_full = rms_scale(hidden_mid, norm_gain)
    normed = normed_full.astype(jnp.bfloat16)
    logits = jnp.dot(normed_full, router_weight, precision=lax.Precision.HIGHEST)
    own_ids = lax.dynamic_slice_in_dim(expert_ids, my_group * row_count, row_count, 0)
    own_onehot = own_ids[:, :, None] == expert_range[None, None, :]
    chosen = jnp.sum(jnp.where(own_onehot, logits[:, None, :], 0.0), axis=-1)
    gate_weights = jax.nn.softmax(chosen, axis=-1)
    gate_hi = gate_weights.astype(jnp.bfloat16)
    gate_lo = (gate_weights - gate_hi.astype(jnp.float32)).astype(jnp.bfloat16)
    side = jnp.concatenate([own_ids.astype(jnp.bfloat16), gate_hi, gate_lo], axis=1)
    side = jnp.pad(side, ((0, 0), (0, 128 - 3 * top_count)))
    packed = lax.all_gather(
        jnp.concatenate([normed, side], axis=1), ("expert", "tensor"), axis=0, tiled=True
    ).reshape(blocks, row_count, model_width + 128)
    all_rows = packed[:, :, :model_width]
    all_ids = packed[:, :, model_width:model_width + top_count].astype(jnp.int32)
    all_hi = packed[:, :, model_width + top_count:model_width + 2 * top_count]
    all_lo = packed[:, :, model_width + 2 * top_count:model_width + 3 * top_count]
    holds = (placement[None, :] == expert_range[:, None]).astype(jnp.int32)
    copies = jnp.sum(holds, axis=1)
    copy_rank = jnp.cumsum(holds, axis=1) - 1
    holder_range = jnp.arange(holders, dtype=jnp.int32)
    copy_pick = holder_range[:, None] % copies[None, :]
    picked = (holds[None] > 0) & (copy_rank[None] == copy_pick[:, :, None])
    slot_pick = jnp.sum(jnp.where(picked, slot_range[None, None, :], 0), axis=2)
    local_range = jnp.arange(slot_dev, dtype=jnp.int32)
    mine_map = (slot_pick[:, :, None] == my_holder * slot_dev + local_range).astype(jnp.bfloat16)
    block_holder = jnp.arange(blocks, dtype=jnp.int32) // groups
    block_map = mine_map[block_holder]
    names = all_ids[:, :, :, None] == expert_range
    name_hot = jnp.any(names, axis=2).astype(jnp.bfloat16)
    gate_e_hi = jnp.sum(jnp.where(names, all_hi[:, :, :, None], 0), axis=2).astype(jnp.bfloat16)
    gate_e_lo = jnp.sum(jnp.where(names, all_lo[:, :, :, None], 0), axis=2).astype(jnp.bfloat16)
    stack = jnp.concatenate([name_hot, gate_e_hi, gate_e_lo], axis=1)
    per_slot = jnp.einsum("bue,bes->bus", stack, block_map, preferred_element_type=jnp.float32)
    token_hit = per_slot[:, :row_count]
    gate_sel_hi = per_slot[:, row_count:2 * row_count]
    gate_sel_lo = per_slot[:, 2 * row_count:]
    token_range = jnp.arange(row_count, dtype=jnp.int32)
    earlier = (token_range[None, :] < token_range[:, None]).astype(jnp.bfloat16)
    count_before = jnp.einsum(
        "uv,bvs->bus", earlier, token_hit.astype(jnp.bfloat16), preferred_element_type=jnp.float32
    )
    rank_range = jnp.arange(capacity, dtype=jnp.float32)
    pick = token_hit[..., None] * (count_before[..., None] == rank_range)
    pick_hot = pick.astype(jnp.bfloat16)
    received = jnp.einsum(
        "busr,bud->sbrd", pick_hot, all_rows, preferred_element_type=jnp.float32
    ).astype(jnp.bfloat16)
    inner_f32 = expert_inner(received, expert_weights)
    if blocks * row_count * model_width * 4 <= (32 << 20):
        gate_sel = gate_sel_hi + gate_sel_lo
        pair_gate = jnp.sum(pick * gate_sel[..., None], axis=1)
        pair_gate = jnp.swapaxes(pair_gate, 0, 1)[..., None]
        inner_act = (inner_f32 * pair_gate).astype(jnp.bfloat16)
        partial_value = expert_down(inner_act, expert_weights).astype(jnp.bfloat16)
        combined = jnp.einsum(
            "busr,sbrd->bud", pick_hot, partial_value, preferred_element_type=jnp.float32
        )
        token_sum = combined.astype(jnp.bfloat16).reshape(holders, groups, row_count, model_width)
        moe_sum = lax.psum_scatter(
            jnp.swapaxes(token_sum, 0, 1).reshape(-1, model_width),
            "tensor",
            scatter_dimension=0,
            tiled=True,
        ).reshape(holders, row_count, model_width)
        moe_sum = lax.all_to_all(moe_sum, "expert", split_axis=0, concat_axis=0, tiled=True)
        moe_sum = jnp.sum(moe_sum.astype(jnp.float32), axis=0)
    else:
        partial_value = expert_down(
            inner_f32.astype(jnp.bfloat16), expert_weights
        ).astype(jnp.bfloat16)
        partial_value = jnp.transpose(
            partial_value.reshape(slot_dev, holders, groups, capacity, model_width), (1, 2, 0, 3, 4)
        )
        expert_sum = lax.psum_scatter(partial_value, "tensor", scatter_dimension=1, tiled=True)
        returned = lax.all_to_all(expert_sum, "expert", split_axis=0, concat_axis=0, tiled=True)
        own_flat = own_ids.reshape(-1)
        own_onehot_flat = own_flat[:, None] == expert_range
        slot_of = jnp.sum(
            jnp.where(own_onehot_flat, slot_pick[my_holder][None, :], 0), axis=-1
        )
        slot_hot = (slot_of[:, None] == slot_range).astype(jnp.int32)
        rank_in = jnp.sum(jnp.cumsum(slot_hot, axis=0) * slot_hot, axis=-1) - 1
        own_index = slot_of * capacity + rank_in
        outputs = returned.reshape(-1, model_width)[own_index].reshape(
            row_count, top_count, model_width
        )
        moe_sum = jnp.einsum("rk,rkd->rd", gate_weights, outputs.astype(jnp.float32))
    hidden_out = hidden_mid + moe_sum
    normed_out = rms_scale(hidden_out, post_gain)
    return (hidden_out, normed_out)


def solution(mesh):
    in_specs = (
        P("expert", "tensor"),
        P("tensor", None),
        P(("expert", "tensor"), None),
        P(),
        P(),
        P("expert", None),
        P(),
        P("expert", None, None, "tensor"),
        P(),
    )
    out_specs = (P(("expert", "tensor"), None), P(("expert", "tensor"), None))
    return jax.shard_map(
        on_device, mesh=mesh, in_specs=in_specs, out_specs=out_specs, check_vma=False
    )
```

```python
import jax
import jax.numpy as jnp
from jax import lax
from jax.sharding import PartitionSpec as P

EPS = 1e-06


def rms_scale(values, gain_row):
    mean_square = jnp.mean(values * values, axis=-1, keepdims=True)
    return values * lax.rsqrt(mean_square + EPS) * gain_row


def expert_inner(block_rows, weights):
    both_pre = jnp.einsum(
        "nqsmd,scdf->nqsmcf", block_rows, weights[:, :2], preferred_element_type=jnp.float32
    )
    return jax.nn.silu(both_pre[..., 0, :]) * both_pre[..., 1, :]


def expert_down(inner_act, weights):
    return jnp.einsum(
        "nqsmf,sdf->nqsmd", inner_act, weights[:, 2], preferred_element_type=jnp.float32
    )


def on_device(
    context,
    out_proj,
    residual,
    norm_gain,
    router_weight,
    expert_ids,
    placement,
    expert_weights,
    post_gain,
):
    groups = lax.axis_size("tensor")
    holders = lax.axis_size("expert")
    my_group = lax.axis_index("tensor")
    my_holder = lax.axis_index("expert")
    row_count = residual.shape[0]
    model_width = residual.shape[1]
    top_count = expert_ids.shape[1]
    expert_count = router_weight.shape[1]
    slot_dev = expert_weights.shape[0]
    slot_total = placement.shape[0]
    blocks = holders * groups
    capacity = max(2, row_count * top_count * 5 // (expert_count * 4))
    expert_range = jnp.arange(expert_count, dtype=jnp.int32)
    slot_range = jnp.arange(slot_total, dtype=jnp.int32)
    attention = lax.psum_scatter(
        jnp.dot(context, out_proj, preferred_element_type=jnp.float32).astype(jnp.bfloat16),
        "tensor",
        scatter_dimension=0,
        tiled=True,
    ).astype(jnp.float32)
    hidden_mid = residual.astype(jnp.float32) + attention
    normed_full = rms_scale(hidden_mid, norm_gain)
    normed = normed_full.astype(jnp.bfloat16)
    logits = jnp.dot(normed_full, router_weight, precision=lax.Precision.HIGHEST)
    own_ids = lax.dynamic_slice_in_dim(expert_ids, my_group * row_count, row_count, 0)
    own_onehot = own_ids[:, :, None] == expert_range[None, None, :]
    chosen = jnp.sum(jnp.where(own_onehot, logits[:, None, :], 0.0), axis=-1)
    gate_weights = jax.nn.softmax(chosen, axis=-1)
    gate_hi = gate_weights.astype(jnp.bfloat16)
    gate_lo = (gate_weights - gate_hi.astype(jnp.float32)).astype(jnp.bfloat16)
    side = jnp.concatenate([own_ids.astype(jnp.bfloat16), gate_hi, gate_lo], axis=1)
    side = jnp.pad(side, ((0, 0), (0, 128 - 3 * top_count)))
    packed = lax.all_gather(
        jnp.concatenate([normed, side], axis=1), ("expert", "tensor"), axis=0, tiled=True
    ).reshape(blocks, row_count, model_width + 128)
    all_rows = packed[:, :, :model_width]
    all_ids = packed[:, :, model_width:model_width + top_count].astype(jnp.int32)
    all_hi = packed[:, :, model_width + top_count:model_width + 2 * top_count]
    all_lo = packed[:, :, model_width + 2 * top_count:model_width + 3 * top_count]
    holds = (placement[None, :] == expert_range[:, None]).astype(jnp.int32)
    copies = jnp.sum(holds, axis=1)
    copy_rank = jnp.cumsum(holds, axis=1) - 1
    holder_range = jnp.arange(holders, dtype=jnp.int32)
    copy_pick = holder_range[:, None] % copies[None, :]
    picked = (holds[None] > 0) & (copy_rank[None] == copy_pick[:, :, None])
    slot_pick = jnp.sum(jnp.where(picked, slot_range[None, None, :], 0), axis=2)
    local_range = jnp.arange(slot_dev, dtype=jnp.int32)
    mine_map = (slot_pick[:, :, None] == my_holder * slot_dev + local_range).astype(jnp.bfloat16)
    block_holder = jnp.arange(blocks, dtype=jnp.int32) // groups
    block_map = mine_map[block_holder]
    names = all_ids[:, :, :, None] == expert_range
    name_hot = jnp.any(names, axis=2).astype(jnp.bfloat16)
    gate_e_hi = jnp.sum(jnp.where(names, all_hi[:, :, :, None], 0), axis=2).astype(jnp.bfloat16)
    gate_e_lo = jnp.sum(jnp.where(names, all_lo[:, :, :, None], 0), axis=2).astype(jnp.bfloat16)
    stack = jnp.concatenate([name_hot, gate_e_hi, gate_e_lo], axis=1)
    per_slot = jnp.einsum("bue,bes->bus", stack, block_map, preferred_element_type=jnp.float32)
    token_hit = per_slot[:, :row_count]
    gate_sel_hi = per_slot[:, row_count:2 * row_count]
    gate_sel_lo = per_slot[:, 2 * row_count:]
    token_range = jnp.arange(row_count, dtype=jnp.int32)
    earlier = (token_range[None, :] < token_range[:, None]).astype(jnp.bfloat16)
    count_before = jnp.einsum(
        "uv,bvs->bus", earlier, token_hit.astype(jnp.bfloat16), preferred_element_type=jnp.float32
    )
    rank_range = jnp.arange(capacity, dtype=jnp.float32)
    pick = token_hit[..., None] * (count_before[..., None] == rank_range)
    pick_hot = pick.astype(jnp.bfloat16)
    received = jnp.einsum(
        "busr,bud->bsrd", pick_hot, all_rows, preferred_element_type=jnp.float32
    ).astype(jnp.bfloat16).reshape(holders, groups, slot_dev, capacity, model_width)
    inner_f32 = expert_inner(received, expert_weights)
    if blocks * row_count * model_width * 4 <= (32 << 20):
        gate_sel = gate_sel_hi + gate_sel_lo
        pair_gate = jnp.sum(pick * gate_sel[..., None], axis=1)
        pair_gate = pair_gate.reshape(holders, groups, slot_dev, capacity, 1)
        inner_act = (inner_f32 * pair_gate).astype(jnp.bfloat16)
        partial_value = expert_down(inner_act, expert_weights).astype(jnp.bfloat16)
        partial_value = partial_value.reshape(blocks, slot_dev, capacity, model_width)
        combined = jnp.einsum(
            "busr,bsrd->bud", pick_hot, partial_value, preferred_element_type=jnp.float32
        )
        token_sum = combined.astype(jnp.bfloat16).reshape(holders, groups, row_count, model_width)
        moe_sum = lax.all_to_all(
            jnp.swapaxes(token_sum, 0, 1), "tensor", split_axis=0, concat_axis=0, tiled=True
        )
        moe_sum = jnp.sum(moe_sum.astype(jnp.float32), axis=0).astype(jnp.bfloat16)
        moe_sum = lax.all_to_all(moe_sum, "expert", split_axis=0, concat_axis=0, tiled=True)
        moe_sum = jnp.sum(moe_sum.astype(jnp.float32), axis=0)
    else:
        partial_value = expert_down(
            inner_f32.astype(jnp.bfloat16), expert_weights
        ).astype(jnp.bfloat16)
        expert_sum = lax.psum_scatter(partial_value, "tensor", scatter_dimension=1, tiled=True)
        returned = lax.all_to_all(expert_sum, "expert", split_axis=0, concat_axis=0, tiled=True)
        own_flat = own_ids.reshape(-1)
        own_onehot_flat = own_flat[:, None] == expert_range
        slot_of = jnp.sum(
            jnp.where(own_onehot_flat, slot_pick[my_holder][None, :], 0), axis=-1
        )
        slot_hot = (slot_of[:, None] == slot_range).astype(jnp.int32)
        rank_in = jnp.sum(jnp.cumsum(slot_hot, axis=0) * slot_hot, axis=-1) - 1
        own_index = slot_of * capacity + rank_in
        outputs = returned.reshape(-1, model_width)[own_index].reshape(
            row_count, top_count, model_width
        )
        moe_sum = jnp.einsum("rk,rkd->rd", gate_weights, outputs.astype(jnp.float32))
    hidden_out = hidden_mid + moe_sum
    normed_out = rms_scale(hidden_out, post_gain)
    return (hidden_out, normed_out)


def solution(mesh):
    in_specs = (
        P("expert", "tensor"),
        P("tensor", None),
        P(("expert", "tensor"), None),
        P(),
        P(),
        P("expert", None),
        P(),
        P("expert", None, None, "tensor"),
        P(),
    )
    out_specs = (P(("expert", "tensor"), None), P(("expert", "tensor"), None))
    return jax.shard_map(
        on_device, mesh=mesh, in_specs=in_specs, out_specs=out_specs, check_vma=False
    )
```

```python
import jax
import jax.numpy as jnp
from jax import lax
from jax.sharding import PartitionSpec as P

EPS = 1e-06


def rms_scale(values, gain_row):
    mean_square = jnp.mean(values * values, axis=-1, keepdims=True)
    return values * lax.rsqrt(mean_square + EPS) * gain_row


def expert_inner(block_rows, weights):
    both_pre = jnp.einsum(
        "nqsmd,scdf->nqsmcf", block_rows, weights[:, :2], preferred_element_type=jnp.float32
    )
    return jax.nn.silu(both_pre[..., 0, :]) * both_pre[..., 1, :]


def expert_down(inner_act, weights):
    return jnp.einsum(
        "nqsmf,sdf->nqsmd", inner_act, weights[:, 2], preferred_element_type=jnp.float32
    )


def on_device(
    context,
    out_proj,
    residual,
    norm_gain,
    router_weight,
    expert_ids,
    placement,
    expert_weights,
    post_gain,
):
    groups = lax.axis_size("tensor")
    holders = lax.axis_size("expert")
    my_group = lax.axis_index("tensor")
    my_holder = lax.axis_index("expert")
    row_count = residual.shape[0]
    model_width = residual.shape[1]
    top_count = expert_ids.shape[1]
    expert_count = router_weight.shape[1]
    slot_dev = expert_weights.shape[0]
    slot_total = placement.shape[0]
    blocks = holders * groups
    capacity = max(2, row_count * top_count * 5 // (expert_count * 4))
    expert_range = jnp.arange(expert_count, dtype=jnp.int32)
    slot_range = jnp.arange(slot_total, dtype=jnp.int32)
    attention_parts = lax.all_to_all(
        jnp.dot(context, out_proj, preferred_element_type=jnp.float32)
        .astype(jnp.bfloat16)
        .reshape(groups, row_count, -1),
        "tensor",
        split_axis=0,
        concat_axis=0,
        tiled=True,
    )
    attention = jnp.sum(attention_parts.astype(jnp.float32), axis=0)
    hidden_mid = residual.astype(jnp.float32) + attention
    normed_full = rms_scale(hidden_mid, norm_gain)
    normed = normed_full.astype(jnp.bfloat16)
    logits = jnp.dot(normed_full, router_weight, precision=lax.Precision.HIGHEST)
    own_ids = lax.dynamic_slice_in_dim(expert_ids, my_group * row_count, row_count, 0)
    own_onehot = own_ids[:, :, None] == expert_range[None, None, :]
    chosen = jnp.sum(jnp.where(own_onehot, logits[:, None, :], 0.0), axis=-1)
    gate_weights = jax.nn.softmax(chosen, axis=-1)
    gate_hi = gate_weights.astype(jnp.bfloat16)
    gate_lo = (gate_weights - gate_hi.astype(jnp.float32)).astype(jnp.bfloat16)
    side = jnp.concatenate([own_ids.astype(jnp.bfloat16), gate_hi, gate_lo], axis=1)
    side = jnp.pad(side, ((0, 0), (0, 128 - 3 * top_count)))
    packed = lax.all_gather(
        jnp.concatenate([normed, side], axis=1), ("expert", "tensor"), axis=0, tiled=True
    ).reshape(blocks, row_count, model_width + 128)
    all_rows = packed[:, :, :model_width]
    all_ids = packed[:, :, model_width:model_width + top_count].astype(jnp.int32)
    all_hi = packed[:, :, model_width + top_count:model_width + 2 * top_count]
    all_lo = packed[:, :, model_width + 2 * top_count:model_width + 3 * top_count]
    holds = (placement[None, :] == expert_range[:, None]).astype(jnp.int32)
    copies = jnp.sum(holds, axis=1)
    copy_rank = jnp.cumsum(holds, axis=1) - 1
    holder_range = jnp.arange(holders, dtype=jnp.int32)
    copy_pick = holder_range[:, None] % copies[None, :]
    picked = (holds[None] > 0) & (copy_rank[None] == copy_pick[:, :, None])
    slot_pick = jnp.sum(jnp.where(picked, slot_range[None, None, :], 0), axis=2)
    local_range = jnp.arange(slot_dev, dtype=jnp.int32)
    mine_map = (slot_pick[:, :, None] == my_holder * slot_dev + local_range).astype(jnp.bfloat16)
    block_holder = jnp.arange(blocks, dtype=jnp.int32) // groups
    block_map = mine_map[block_holder]
    names = all_ids[:, :, :, None] == expert_range
    name_hot = jnp.any(names, axis=2).astype(jnp.bfloat16)
    gate_e_hi = jnp.sum(jnp.where(names, all_hi[:, :, :, None], 0), axis=2).astype(jnp.bfloat16)
    gate_e_lo = jnp.sum(jnp.where(names, all_lo[:, :, :, None], 0), axis=2).astype(jnp.bfloat16)
    stack = jnp.concatenate([name_hot, gate_e_hi, gate_e_lo], axis=1)
    per_slot = jnp.einsum("bue,bes->bus", stack, block_map, preferred_element_type=jnp.float32)
    token_hit = per_slot[:, :row_count]
    gate_sel_hi = per_slot[:, row_count:2 * row_count]
    gate_sel_lo = per_slot[:, 2 * row_count:]
    token_range = jnp.arange(row_count, dtype=jnp.int32)
    earlier = (token_range[None, :] < token_range[:, None]).astype(jnp.bfloat16)
    count_before = jnp.einsum(
        "uv,bvs->bus", earlier, token_hit.astype(jnp.bfloat16), preferred_element_type=jnp.float32
    )
    rank_range = jnp.arange(capacity, dtype=jnp.float32)
    pick = token_hit[..., None] * (count_before[..., None] == rank_range)
    pick_hot = pick.astype(jnp.bfloat16)
    received = jnp.einsum(
        "busr,bud->bsrd", pick_hot, all_rows, preferred_element_type=jnp.float32
    ).astype(jnp.bfloat16).reshape(holders, groups, slot_dev, capacity, model_width)
    inner_f32 = expert_inner(received, expert_weights)
    if blocks * row_count * model_width * 4 <= (32 << 20):
        gate_sel = gate_sel_hi + gate_sel_lo
        pair_gate = jnp.sum(pick * gate_sel[..., None], axis=1)
        pair_gate = pair_gate.reshape(holders, groups, slot_dev, capacity, 1)
        inner_act = (inner_f32 * pair_gate).astype(jnp.bfloat16)
        partial_value = expert_down(inner_act, expert_weights).astype(jnp.bfloat16)
        partial_value = partial_value.reshape(blocks, slot_dev, capacity, model_width)
        combined = jnp.einsum(
            "busr,bsrd->bud", pick_hot, partial_value, preferred_element_type=jnp.float32
        )
        token_sum = combined.astype(jnp.bfloat16).reshape(holders, groups, row_count, model_width)
        moe_sum = lax.psum_scatter(
            jnp.swapaxes(token_sum, 0, 1).reshape(-1, model_width),
            "tensor",
            scatter_dimension=0,
            tiled=True,
        ).reshape(holders, row_count, model_width)
        moe_sum = lax.all_to_all(moe_sum, "expert", split_axis=0, concat_axis=0, tiled=True)
        moe_sum = jnp.sum(moe_sum.astype(jnp.float32), axis=0)
    else:
        partial_value = expert_down(
            inner_f32.astype(jnp.bfloat16), expert_weights
        ).astype(jnp.bfloat16)
        expert_sum = lax.psum_scatter(partial_value, "tensor", scatter_dimension=1, tiled=True)
        returned = lax.all_to_all(expert_sum, "expert", split_axis=0, concat_axis=0, tiled=True)
        own_flat = own_ids.reshape(-1)
        own_onehot_flat = own_flat[:, None] == expert_range
        slot_of = jnp.sum(
            jnp.where(own_onehot_flat, slot_pick[my_holder][None, :], 0), axis=-1
        )
        slot_hot = (slot_of[:, None] == slot_range).astype(jnp.int32)
        rank_in = jnp.sum(jnp.cumsum(slot_hot, axis=0) * slot_hot, axis=-1) - 1
        own_index = slot_of * capacity + rank_in
        outputs = returned.reshape(-1, model_width)[own_index].reshape(
            row_count, top_count, model_width
        )
        moe_sum = jnp.einsum("rk,rkd->rd", gate_weights, outputs.astype(jnp.float32))
    hidden_out = hidden_mid + moe_sum
    normed_out = rms_scale(hidden_out, post_gain)
    return (hidden_out, normed_out)


def solution(mesh):
    in_specs = (
        P("expert", "tensor"),
        P("tensor", None),
        P(("expert", "tensor"), None),
        P(),
        P(),
        P("expert", None),
        P(),
        P("expert", None, None, "tensor"),
        P(),
    )
    out_specs = (P(("expert", "tensor"), None), P(("expert", "tensor"), None))
    return jax.shard_map(
        on_device, mesh=mesh, in_specs=in_specs, out_specs=out_specs, check_vma=False
    )
```

```python
import jax
import jax.numpy as jnp
from jax import lax
from jax.sharding import PartitionSpec as P

EPS = 1e-06


def rms_scale(values, gain_row):
    mean_square = jnp.mean(values * values, axis=-1, keepdims=True)
    return values * lax.rsqrt(mean_square + EPS) * gain_row


def expert_inner(block_rows, weights):
    both_pre = jnp.einsum(
        "nqsmd,scdf->nqsmcf", block_rows, weights[:, :2], preferred_element_type=jnp.float32
    )
    return jax.nn.silu(both_pre[..., 0, :]) * both_pre[..., 1, :]


def expert_down(inner_act, weights):
    return jnp.einsum(
        "nqsmf,sdf->nqsmd", inner_act, weights[:, 2], preferred_element_type=jnp.float32
    )


def on_device(
    context,
    out_proj,
    residual,
    norm_gain,
    router_weight,
    expert_ids,
    placement,
    expert_weights,
    post_gain,
):
    groups = lax.axis_size("tensor")
    holders = lax.axis_size("expert")
    my_group = lax.axis_index("tensor")
    my_holder = lax.axis_index("expert")
    row_count = residual.shape[0]
    model_width = residual.shape[1]
    top_count = expert_ids.shape[1]
    expert_count = router_weight.shape[1]
    slot_dev = expert_weights.shape[0]
    slot_total = placement.shape[0]
    blocks = holders * groups
    capacity = max(2, row_count * top_count * 5 // (expert_count * 4))
    expert_range = jnp.arange(expert_count, dtype=jnp.int32)
    slot_range = jnp.arange(slot_total, dtype=jnp.int32)
    attention_parts = lax.all_to_all(
        jnp.dot(context, out_proj, preferred_element_type=jnp.float32)
        .astype(jnp.bfloat16)
        .reshape(groups, row_count, -1),
        "tensor",
        split_axis=0,
        concat_axis=0,
        tiled=True,
    )
    attention = jnp.sum(attention_parts.astype(jnp.float32), axis=0)
    hidden_mid = residual.astype(jnp.float32) + attention
    normed_full = rms_scale(hidden_mid, norm_gain)
    normed = normed_full.astype(jnp.bfloat16)
    logits = jnp.dot(normed_full, router_weight, precision=lax.Precision.HIGHEST)
    own_ids = lax.dynamic_slice_in_dim(expert_ids, my_group * row_count, row_count, 0)
    own_onehot = own_ids[:, :, None] == expert_range[None, None, :]
    chosen = jnp.sum(jnp.where(own_onehot, logits[:, None, :], 0.0), axis=-1)
    gate_weights = jax.nn.softmax(chosen, axis=-1)
    gate_hi = gate_weights.astype(jnp.bfloat16)
    gate_lo = (gate_weights - gate_hi.astype(jnp.float32)).astype(jnp.bfloat16)
    side = jnp.concatenate([own_ids.astype(jnp.bfloat16), gate_hi, gate_lo], axis=1)
    side = jnp.pad(side, ((0, 0), (0, 128 - 3 * top_count)))
    packed = lax.all_gather(
        jnp.concatenate([normed, side], axis=1), ("expert", "tensor"), axis=0, tiled=True
    ).reshape(blocks, row_count, model_width + 128)
    all_rows = packed[:, :, :model_width]
    all_ids = packed[:, :, model_width:model_width + top_count].astype(jnp.int32)
    all_hi = packed[:, :, model_width + top_count:model_width + 2 * top_count]
    all_lo = packed[:, :, model_width + 2 * top_count:model_width + 3 * top_count]
    holds = (placement[None, :] == expert_range[:, None]).astype(jnp.int32)
    copies = jnp.sum(holds, axis=1)
    copy_rank = jnp.cumsum(holds, axis=1) - 1
    holder_range = jnp.arange(holders, dtype=jnp.int32)
    copy_pick = holder_range[:, None] % copies[None, :]
    picked = (holds[None] > 0) & (copy_rank[None] == copy_pick[:, :, None])
    slot_pick = jnp.sum(jnp.where(picked, slot_range[None, None, :], 0), axis=2)
    local_range = jnp.arange(slot_dev, dtype=jnp.int32)
    mine_map = (slot_pick[:, :, None] == my_holder * slot_dev + local_range).astype(jnp.bfloat16)
    block_holder = jnp.arange(blocks, dtype=jnp.int32) // groups
    block_map = mine_map[block_holder]
    names = all_ids[:, :, :, None] == expert_range
    name_hot = jnp.any(names, axis=2).astype(jnp.bfloat16)
    gate_e_hi = jnp.sum(jnp.where(names, all_hi[:, :, :, None], 0), axis=2).astype(jnp.bfloat16)
    gate_e_lo = jnp.sum(jnp.where(names, all_lo[:, :, :, None], 0), axis=2).astype(jnp.bfloat16)
    stack = jnp.concatenate([name_hot, gate_e_hi, gate_e_lo], axis=1)
    per_slot = jnp.einsum("bue,bes->bus", stack, block_map, preferred_element_type=jnp.float32)
    token_hit = per_slot[:, :row_count]
    gate_sel_hi = per_slot[:, row_count:2 * row_count]
    gate_sel_lo = per_slot[:, 2 * row_count:]
    token_range = jnp.arange(row_count, dtype=jnp.int32)
    earlier = (token_range[None, :] < token_range[:, None]).astype(jnp.bfloat16)
    count_before = jnp.einsum(
        "uv,bvs->bus", earlier, token_hit.astype(jnp.bfloat16), preferred_element_type=jnp.float32
    )
    rank_range = jnp.arange(capacity, dtype=jnp.float32)
    pick = token_hit[..., None] * (count_before[..., None] == rank_range)
    pick_hot = pick.astype(jnp.bfloat16)
    received = jnp.einsum(
        "busr,bud->bsrd", pick_hot, all_rows, preferred_element_type=jnp.float32
    ).astype(jnp.bfloat16).reshape(holders, groups, slot_dev, capacity, model_width)
    inner_f32 = expert_inner(received, expert_weights)
    if blocks * row_count * model_width * 4 <= (32 << 20):
        gate_sel = gate_sel_hi + gate_sel_lo
        pair_gate = jnp.sum(pick * gate_sel[..., None], axis=1)
        pair_gate = pair_gate.reshape(holders, groups, slot_dev, capacity, 1)
        inner_act = (inner_f32 * pair_gate).astype(jnp.bfloat16)
        partial_value = expert_down(inner_act, expert_weights).astype(jnp.bfloat16)
        partial_value = partial_value.reshape(blocks, slot_dev, capacity, model_width)
        combined = jnp.einsum(
            "hqusr,hqsrd->qhud",
            pick_hot.reshape(holders, groups, row_count, slot_dev, capacity),
            partial_value.reshape(holders, groups, slot_dev, capacity, model_width),
            preferred_element_type=jnp.float32,
        )
        moe_sum = lax.psum_scatter(
            combined.astype(jnp.bfloat16).reshape(-1, model_width),
            "tensor",
            scatter_dimension=0,
            tiled=True,
        ).reshape(holders, row_count, model_width)
        moe_sum = lax.all_to_all(moe_sum, "expert", split_axis=0, concat_axis=0, tiled=True)
        moe_sum = jnp.sum(moe_sum.astype(jnp.float32), axis=0)
    else:
        partial_value = expert_down(
            inner_f32.astype(jnp.bfloat16), expert_weights
        ).astype(jnp.bfloat16)
        expert_sum = lax.psum_scatter(partial_value, "tensor", scatter_dimension=1, tiled=True)
        returned = lax.all_to_all(expert_sum, "expert", split_axis=0, concat_axis=0, tiled=True)
        own_flat = own_ids.reshape(-1)
        own_onehot_flat = own_flat[:, None] == expert_range
        slot_of = jnp.sum(
            jnp.where(own_onehot_flat, slot_pick[my_holder][None, :], 0), axis=-1
        )
        slot_hot = (slot_of[:, None] == slot_range).astype(jnp.int32)
        rank_in = jnp.sum(jnp.cumsum(slot_hot, axis=0) * slot_hot, axis=-1) - 1
        own_index = slot_of * capacity + rank_in
        outputs = returned.reshape(-1, model_width)[own_index].reshape(
            row_count, top_count, model_width
        )
        moe_sum = jnp.einsum("rk,rkd->rd", gate_weights, outputs.astype(jnp.float32))
    hidden_out = hidden_mid + moe_sum
    normed_out = rms_scale(hidden_out, post_gain)
    return (hidden_out, normed_out)


def solution(mesh):
    in_specs = (
        P("expert", "tensor"),
        P("tensor", None),
        P(("expert", "tensor"), None),
        P(),
        P(),
        P("expert", None),
        P(),
        P("expert", None, None, "tensor"),
        P(),
    )
    out_specs = (P(("expert", "tensor"), None), P(("expert", "tensor"), None))
    return jax.shard_map(
        on_device, mesh=mesh, in_specs=in_specs, out_specs=out_specs, check_vma=False
    )
```
